32 devices in a mesh: gx: 8 (over z, x), wl: 4 (over y, core).
Axes of the slice: x: 2, y: 2, z: 4, core: 2. Of those that a mesh axis runs over, the one named last changes fastest.
Arguments:
- beam_field: float32 [512, 32, 2, 1024], P('gx', 'wl'), may hold values from -6 to 6
- region_labels: int32 [512, 1024], P('gx'), may hold values from 0 to 15
- gain_table: float32 [16], replicated, may hold values from 0.5 to 4
- diffraction: float32 [32], P('wl'), may hold values from 1000 to 4000
- spectral_weight: float32 [32], P('wl'), may hold values from 0.6 to 4.8
Outputs:
- field_out: float32 [512, 32, 2, 1024], P('gx', 'wl')
- gain_out: float32 [512, 1024], P('gx')
The draws below stay inside these ranges and needn't reach their ends.
All inputs are finite; a program needn't handle non-finite values.
Results may differ from the reference program's by a relative error of at most 0.0004.
Values sent between devices are 32-bit elements; how exact they have to be, the bound alone decides.
No kernel may reach another device: no remote copies, remote signals or barrier semaphores. Data moves between devices by JAX's collectives and lax.ppermute only.
A program may use at most 128 MiB of HBM per device.

```python
import math
import jax
import jax.numpy as jnp
from jax import lax

NY = 1024
REGIONS = 16
NX = 512
WL = 32


def draw_spectral_weight(key, part):
    counter = jnp.arange(WL, dtype=jnp.float32)
    rising = 1.0 + 2.0 * counter / max(WL - 1, 1)
    factor = jax.random.uniform(key, (WL,), jnp.float32, 0.7, 1.4)
    return rising * factor


def plant(array, own_key, low, high):
    spot = [jax.random.randint(jax.random.fold_in(own_key, axis), (), 0, length) for axis, length in enumerate(array.shape)]
    widest = array.shape.index(max(array.shape))
    beside = spot[:widest] + [(spot[widest] + 1) % array.shape[widest]] + spot[widest + 1:]
    return array.at[tuple(spot)].set(low).at[tuple(beside)].set(high)


def block_scale(own_key, shape, cuts, least, largest):
    def one(position, blocks):
        heights = jax.random.uniform(jax.random.fold_in(jax.random.fold_in(own_key, 6), position), (blocks,), jnp.float32, least / len(cuts), largest / len(cuts))
        return jnp.repeat(jnp.exp(heights), shape[position] // blocks).reshape((-1,) + (1,) * (len(shape) - position - 1))

    gain = one(*cuts[0])
    for cut in cuts[1:]:
        gain = gain * one(*cut)
    return gain


def scatter_about(own_key, dims, spread, limit, pieces=(), held_as=jnp.bfloat16):
    drawn = spread * jax.random.normal(own_key, dims, jnp.float32)
    if pieces:
        drawn = drawn * block_scale(own_key, dims, pieces, -0.22, 0.18)
    return jnp.clip(drawn, -limit, limit).astype(held_as)


def setup_inputs(seed: int = 0) -> dict:
    key_list = jax.random.split(jax.random.key(seed), 6)
    beam_field = scatter_about(key_list[0], (NX, WL, 2, NY), 1.0, 6.0, ((0, 8), (1, 4)), jnp.float32)
    region_labels = plant(jax.random.randint(key_list[1], (NX, NY), 0, REGIONS), jax.random.fold_in(key_list[1], 1), 0, REGIONS - 1).astype(jnp.int32)
    gain_table = jnp.clip(jnp.exp(jax.random.uniform(key_list[2], (REGIONS,), jnp.float32, math.log(0.5), math.log(4.0))), 0.5, 4.0)
    diffraction = jnp.clip(jnp.exp(math.log(4000.0) - 1.3862944 * jax.random.uniform(key_list[3], (WL,), jnp.float32) ** block_scale(key_list[3], (WL,), ((0, 4),), -0.2, 0.2)), 1000.0, 4000.0)
    spectral_weight = draw_spectral_weight(jax.random.fold_in(key_list[5], 71), 0)
    return dict(beam_field=beam_field, region_labels=region_labels, gain_table=gain_table, diffraction=diffraction, spectral_weight=spectral_weight)


def complex_div(top_re, top_im, bottom_re, bottom_im):
    magnitude = bottom_re * bottom_re + bottom_im * bottom_im
    return (top_re * bottom_re + top_im * bottom_im) / magnitude, (top_im * bottom_re - top_re * bottom_im) / magnitude


def apply_explicit(source, laplace, coefficient):
    factor = coefficient[None, :, None]
    real_part = source[:, :, 0] - factor * laplace[:, :, 1]
    imag_part = source[:, :, 1] + factor * laplace[:, :, 0]
    return jnp.stack([real_part, imag_part], axis=2)


def sweep_solve(rhs_re, rhs_im, coefficient):
    zeros = jnp.zeros_like(rhs_re[0])

    def forward_row(carry, row_pair):
        prev_cr, prev_ci, prev_dr, prev_di = carry
        row_re, row_im = row_pair
        pivot_re = 1.0 - coefficient * prev_ci
        pivot_im = 2.0 * coefficient + coefficient * prev_cr
        magnitude = pivot_re * pivot_re + pivot_im * pivot_im
        next_cr = -coefficient * pivot_im / magnitude
        next_ci = -coefficient * pivot_re / magnitude
        next_dr, next_di = complex_div(row_re - coefficient * prev_di, row_im + coefficient * prev_dr, pivot_re, pivot_im)
        state = (next_cr, next_ci, next_dr, next_di)
        return state, state

    final_carry, stacked = lax.scan(forward_row, (zeros, zeros, zeros, zeros), (rhs_re, rhs_im))

    def backward_row(carry, row_set):
        next_re, next_im = carry
        sweep_cr, sweep_ci, sweep_dr, sweep_di = row_set
        value_re = sweep_dr - (sweep_cr * next_re - sweep_ci * next_im)
        value_im = sweep_di - (sweep_cr * next_im + sweep_ci * next_re)
        return (value_re, value_im), (value_re, value_im)

    final_back, solution = lax.scan(backward_row, (zeros, zeros), stacked, reverse=True)
    return solution


def reference(beam_field, region_labels, gain_table, diffraction, spectral_weight):
    base_gain = gain_table[region_labels]

    def saturated(values):
        fluence = jnp.sum(spectral_weight[None, :, None] * (values[:, :, 0] * values[:, :, 0] + values[:, :, 1] * values[:, :, 1]), axis=1)
        return base_gain / (1.0 + fluence / WL)

    gain_in = saturated(beam_field)
    amplified = beam_field * jnp.exp(0.5 * gain_in)[:, None, None, :]
    padded = jnp.pad(amplified, ((0, 0), (0, 0), (0, 0), (1, 1)))
    laplace = (padded[..., 2:] + padded[..., :-2]) - 2.0 * amplified
    driven = apply_explicit(amplified, laplace, diffraction)
    solved_re, solved_im = sweep_solve(driven[:, :, 0], driven[:, :, 1], diffraction[:, None])
    solved = jnp.stack([solved_re, solved_im], axis=2)
    second = 2.0 * solved - driven
    rows_re = jnp.transpose(second[:, :, 0], (2, 0, 1))
    rows_im = jnp.transpose(second[:, :, 1], (2, 0, 1))
    result_re, result_im = sweep_solve(rows_re, rows_im, diffraction[None, :])
    result = jnp.stack([jnp.transpose(result_re, (1, 2, 0)), jnp.transpose(result_im, (1, 2, 0))], axis=2)
    gain_out = saturated(result)
    return result * jnp.exp(0.5 * gain_out)[:, None, None, :], gain_out
```

```python
import math

import jax
import jax.numpy as jnp
from jax import lax
from jax.sharding import PartitionSpec as P

HIGHEST = lax.Precision.HIGHEST
HIGH = lax.Precision.HIGH


def complex_multiply(left_re, left_im, right_re, right_im):
    return (left_re * right_re - left_im * right_im, left_re * right_im + left_im * right_re)


def complex_div(top_re, top_im, bottom_re, bottom_im):
    magnitude = bottom_re * bottom_re + bottom_im * bottom_im
    return (
        (top_re * bottom_re + top_im * bottom_im) / magnitude,
        (top_im * bottom_re - top_re * bottom_im) / magnitude,
    )


def sine_rows(index, length):
    mode = jnp.arange(1, length + 1, dtype=jnp.int32)
    product = ((index + 1)[:, None] * mode[None, :]) % (2 * (length + 1))
    value = jnp.sin(product.astype(jnp.float32) * (math.pi / (length + 1))) * math.sqrt(
        2.0 / (length + 1)
    )
    inside = ((index >= 0) & (index < length))[:, None]
    return jnp.where(inside, value, 0.0)


def eigen_scaled(length, diffraction):
    counter = jnp.arange(1, length + 1, dtype=jnp.float32)
    eigenvalue = 4.0 * jnp.sin(counter * (math.pi / (2 * (length + 1)))) ** 2
    return diffraction[:, None] * eigenvalue[None, :]


def inverse_factor(length, diffraction):
    scaled = eigen_scaled(length, diffraction)
    magnitude = 1.0 + scaled * scaled
    return 1.0 / magnitude, -scaled / magnitude


def cayley_factor(length, diffraction):
    scaled = eigen_scaled(length, diffraction)
    magnitude = 1.0 + scaled * scaled
    return (1.0 - scaled * scaled) / magnitude, -2.0 * scaled / magnitude


def butterfly_sum(value, axis):
    count = lax.axis_size(axis)
    if count & (count - 1):
        return lax.psum(value, axis)
    step = 1
    while step < count:
        pairs = [(i, i ^ step) for i in range(count)]
        value = value + lax.ppermute(value, axis, pairs)
        step *= 2
    return value


def shifted(value, axis, offset):
    count = lax.axis_size(axis)
    pairs = [(i, i + offset) for i in range(count) if 0 <= i + offset < count]
    return jax.tree.map(lambda part: lax.ppermute(part, axis, pairs), value)


def green_entries(rows, cols, factor_re, factor_im, length):
    row_table = sine_rows(rows, length)
    col_table = sine_rows(cols, length)
    both = row_table * col_table
    return (
        jnp.einsum("mn,wn->wm", both, factor_re, precision=HIGHEST),
        jnp.einsum("mn,wn->wm", both, factor_im, precision=HIGHEST),
    )


def safe_ratio(top_re, top_im, bottom_re, bottom_im):
    empty = (bottom_re == 0.0) & (bottom_im == 0.0)
    ratio_re, ratio_im = complex_div(
        top_re, top_im, jnp.where(empty, 1.0, bottom_re), bottom_im
    )
    return jnp.where(empty, 0.0, ratio_re), jnp.where(empty, 0.0, ratio_im)


def cayley_rows(values, table, phase_re, phase_im):
    spectrum = jnp.dot(values, table, precision=HIGH)
    mixed_re, mixed_im = complex_multiply(
        spectrum[..., 0, :], spectrum[..., 1, :], phase_re, phase_im
    )
    return jnp.dot(jnp.stack([mixed_re, mixed_im], axis=-2), table, precision=HIGH)


def shards(beam_field, region_labels, gain_table, diffraction, spectral_weight):
    block, spectra_dev, _, columns = beam_field.shape
    spectra = spectra_dev * lax.axis_size("wl")
    count = lax.axis_size("gx")
    me = lax.axis_index("gx")
    cells = block * count
    regions = gain_table.shape[0]
    region_index = jnp.arange(regions, dtype=jnp.int32)
    base_gain = jnp.sum(
        jnp.where(
            region_labels[None] == region_index[:, None, None], gain_table[:, None, None], 0.0
        ),
        axis=0,
    )

    def power_sum(values):
        return jnp.sum(
            spectral_weight[None, :, None]
            * (values[:, :, 0] * values[:, :, 0] + values[:, :, 1] * values[:, :, 1]),
            axis=1,
        )

    fluence_in = butterfly_sum(power_sum(beam_field), "wl")
    gain_in = base_gain / (1.0 + fluence_in / spectra)
    amplified = beam_field * jnp.exp(0.5 * gain_in)[:, None, None, :]

    factor_re, factor_im = inverse_factor(cells, diffraction)
    start = me * block
    around = start - 1 + jnp.arange(block + 2, dtype=jnp.int32)
    around_table = sine_rows(around, cells)
    green_re = jnp.einsum(
        "an,wn,bn->wab", around_table, factor_re, around_table, precision=HIGHEST
    )
    green_im = jnp.einsum(
        "an,wn,bn->wab", around_table, factor_im, around_table, precision=HIGHEST
    )

    def apply_block(rows_re, rows_im, values):
        kernel = jnp.stack(
            [
                jnp.stack([rows_re, -rows_im], axis=2),
                jnp.stack([rows_im, rows_re], axis=2),
            ],
            axis=1,
        )
        return jnp.einsum("wdack,kwcy->awdy", kernel, values, precision=HIGHEST)

    edge_rows = jnp.array([0, block + 1], dtype=jnp.int32)
    edge_re = green_re[:, edge_rows, 1 : block + 1]
    edge_im = green_im[:, edge_rows, 1 : block + 1]
    edges = apply_block(edge_re, edge_im, amplified)
    to_left = (edges[0, :, 0], edges[0, :, 1])
    to_right = (edges[1, :, 0], edges[1, :, 1])

    block_index = jnp.arange(count, dtype=jnp.int32)
    starts = block_index * block
    ends = starts + block - 1
    rise_re, rise_im = safe_ratio(
        *green_entries(starts + block, starts - 1, factor_re, factor_im, cells),
        *green_entries(starts, starts - 1, factor_re, factor_im, cells),
    )
    fall_re, fall_im = safe_ratio(
        *green_entries(ends - block, ends + 1, factor_re, factor_im, cells),
        *green_entries(ends, ends + 1, factor_re, factor_im, cells),
    )

    def span_product(ratio_re, ratio_im, first, length):
        total_re = jnp.ones_like(ratio_re[:, 0])
        total_im = jnp.zeros_like(ratio_im[:, 0])
        for offset in range(length):
            pick = jnp.clip(first + offset, 0, count - 1)
            total_re, total_im = complex_multiply(
                total_re, total_im, ratio_re[:, pick], ratio_im[:, pick]
            )
        return total_re[:, None], total_im[:, None]

    left_re, left_im = shifted(to_right, "gx", 1)
    right_re, right_im = shifted(to_left, "gx", -1)
    span = 1
    while span < count - 1:
        far_left = shifted((left_re, left_im), "gx", span)
        far_right = shifted((right_re, right_im), "gx", -span)
        gain_re, gain_im = span_product(rise_re, rise_im, me - span, span)
        moved = complex_multiply(gain_re, gain_im, far_left[0], far_left[1])
        left_re, left_im = left_re + moved[0], left_im + moved[1]
        gain_re, gain_im = span_product(fall_re, fall_im, me + 1, span)
        moved = complex_multiply(gain_re, gain_im, far_right[0], far_right[1])
        right_re, right_im = right_re + moved[0], right_im + moved[1]
        span *= 2

    table_rows = sine_rows(lax.optimization_barrier(jnp.arange(columns, dtype=jnp.int32)), columns)
    phase_re, phase_im = cayley_factor(columns, diffraction)
    along_y = cayley_rows(amplified, table_rows, phase_re, phase_im)
    carried = cayley_rows(
        jnp.stack(
            [jnp.stack([left_re, left_im], axis=1), jnp.stack([right_re, right_im], axis=1)]
        ),
        table_rows,
        phase_re,
        phase_im,
    )

    local = apply_block(
        green_re[:, 1 : block + 1, 1 : block + 1], green_im[:, 1 : block + 1, 1 : block + 1], along_y
    )
    from_left = safe_ratio(
        green_re[:, 1 : block + 1, 0],
        green_im[:, 1 : block + 1, 0],
        green_re[:, 1:2, 0],
        green_im[:, 1:2, 0],
    )
    from_right = safe_ratio(
        green_re[:, 1 : block + 1, block + 1],
        green_im[:, 1 : block + 1, block + 1],
        green_re[:, block : block + 1, block + 1],
        green_im[:, block : block + 1, block + 1],
    )
    lead = complex_multiply(
        from_left[0].T[:, :, None],
        from_left[1].T[:, :, None],
        carried[0, :, 0][None],
        carried[0, :, 1][None],
    )
    trail = complex_multiply(
        from_right[0].T[:, :, None],
        from_right[1].T[:, :, None],
        carried[1, :, 0][None],
        carried[1, :, 1][None],
    )
    solved = local + jnp.stack([lead[0] + trail[0], lead[1] + trail[1]], axis=2)
    result = 2.0 * solved - along_y

    fluence_out = butterfly_sum(power_sum(result), "wl")
    gain_out = base_gain / (1.0 + fluence_out / spectra)
    return (result * jnp.exp(0.5 * gain_out)[:, None, None, :], gain_out)


def solution(mesh):
    placed = (P("gx", "wl", None, None), P("gx", None), P(), P("wl"), P("wl"))
    return jax.shard_map(
        shards,
        mesh=mesh,
        in_specs=placed,
        out_specs=(P("gx", "wl", None, None), P("gx", None)),
        check_vma=False,
    )
```

```python
import math

import jax
import jax.numpy as jnp
from jax import lax
from jax.sharding import PartitionSpec as P

HIGHEST = lax.Precision.HIGHEST
HIGH = lax.Precision.HIGH


def complex_multiply(left_re, left_im, right_re, right_im):
    return (left_re * right_re - left_im * right_im, left_re * right_im + left_im * right_re)


def complex_div(top_re, top_im, bottom_re, bottom_im):
    magnitude = bottom_re * bottom_re + bottom_im * bottom_im
    return (
        (top_re * bottom_re + top_im * bottom_im) / magnitude,
        (top_im * bottom_re - top_re * bottom_im) / magnitude,
    )


def sine_rows(index, length):
    mode = jnp.arange(1, length + 1, dtype=jnp.int32)
    product = ((index + 1)[:, None] * mode[None, :]) % (2 * (length + 1))
    value = jnp.sin(product.astype(jnp.float32) * (math.pi / (length + 1))) * math.sqrt(
        2.0 / (length + 1)
    )
    inside = ((index >= 0) & (index < length))[:, None]
    return jnp.where(inside, value, 0.0)


def eigen_scaled(length, diffraction):
    counter = jnp.arange(1, length + 1, dtype=jnp.float32)
    eigenvalue = 4.0 * jnp.sin(counter * (math.pi / (2 * (length + 1)))) ** 2
    return diffraction[:, None] * eigenvalue[None, :]


def inverse_factor(length, diffraction):
    scaled = eigen_scaled(length, diffraction)
    magnitude = 1.0 + scaled * scaled
    return 1.0 / magnitude, -scaled / magnitude


def cayley_factor(length, diffraction):
    scaled = eigen_scaled(length, diffraction)
    magnitude = 1.0 + scaled * scaled
    return (1.0 - scaled * scaled) / magnitude, -2.0 * scaled / magnitude


def butterfly_sum(value, axis):
    count = lax.axis_size(axis)
    if count & (count - 1):
        return lax.psum(value, axis)
    step = 1
    while step < count:
        pairs = [(i, i ^ step) for i in range(count)]
        value = value + lax.ppermute(value, axis, pairs)
        step *= 2
    return value


def shifted(value, axis, offset):
    count = lax.axis_size(axis)
    pairs = [(i, i + offset) for i in range(count) if 0 <= i + offset < count]
    return jax.tree.map(lambda part: lax.ppermute(part, axis, pairs), value)


def green_entries(rows, cols, factor_re, factor_im, length):
    row_table = sine_rows(rows, length)
    col_table = sine_rows(cols, length)
    both = row_table * col_table
    return (
        jnp.einsum("mn,wn->wm", both, factor_re, precision=HIGHEST),
        jnp.einsum("mn,wn->wm", both, factor_im, precision=HIGHEST),
    )


def safe_ratio(top_re, top_im, bottom_re, bottom_im):
    empty = (bottom_re == 0.0) & (bottom_im == 0.0)
    ratio_re, ratio_im = complex_div(
        top_re, top_im, jnp.where(empty, 1.0, bottom_re), bottom_im
    )
    return jnp.where(empty, 0.0, ratio_re), jnp.where(empty, 0.0, ratio_im)


def cayley_rows(values, table, phase_re, phase_im):
    spectrum = jnp.dot(values, table, precision=HIGH)
    mixed_re, mixed_im = complex_multiply(
        spectrum[..., 0, :], spectrum[..., 1, :], phase_re, phase_im
    )
    return jnp.dot(jnp.stack([mixed_re, mixed_im], axis=-2), table, precision=HIGH)


def shards(beam_field, region_labels, gain_table, diffraction, spectral_weight):
    block, spectra_dev, _, columns = beam_field.shape
    spectra = spectra_dev * lax.axis_size("wl")
    count = lax.axis_size("gx")
    me = lax.axis_index("gx")
    cells = block * count
    regions = gain_table.shape[0]
    region_index = jnp.arange(regions, dtype=jnp.int32)
    base_gain = jnp.sum(
        jnp.where(
            region_labels[None] == region_index[:, None, None], gain_table[:, None, None], 0.0
        ),
        axis=0,
    )

    def power_sum(values):
        return jnp.sum(spectral_weight[None, :, None, None] * (values * values), axis=(1, 2))

    fluence_in = butterfly_sum(power_sum(beam_field), "wl")
    gain_in = base_gain / (1.0 + fluence_in / spectra)
    amplified = beam_field * jnp.exp(0.5 * gain_in)[:, None, None, :]

    factor_re, factor_im = inverse_factor(cells, diffraction)
    start = me * block
    around = start - 1 + jnp.arange(block + 2, dtype=jnp.int32)
    around_table = sine_rows(around, cells)
    green_re = jnp.einsum(
        "an,wn,bn->wab", around_table, factor_re, around_table, precision=HIGHEST
    )
    green_im = jnp.einsum(
        "an,wn,bn->wab", around_table, factor_im, around_table, precision=HIGHEST
    )

    def apply_block(rows_re, rows_im, values):
        kernel = jnp.stack(
            [
                jnp.stack([rows_re, -rows_im], axis=2),
                jnp.stack([rows_im, rows_re], axis=2),
            ],
            axis=1,
        )
        return jnp.einsum("wdack,kwcy->awdy", kernel, values, precision=HIGHEST)

    block_index = jnp.arange(count, dtype=jnp.int32)
    starts = block_index * block
    ends = starts + block - 1
    rise_re, rise_im = safe_ratio(
        *green_entries(starts + block, starts - 1, factor_re, factor_im, cells),
        *green_entries(starts, starts - 1, factor_re, factor_im, cells),
    )
    fall_re, fall_im = safe_ratio(
        *green_entries(ends - block, ends + 1, factor_re, factor_im, cells),
        *green_entries(ends, ends + 1, factor_re, factor_im, cells),
    )

    def span_product(ratio_re, ratio_im, first, length):
        total_re = jnp.ones_like(ratio_re[:, 0])
        total_im = jnp.zeros_like(ratio_im[:, 0])
        for offset in range(length):
            pick = jnp.clip(first + offset, 0, count - 1)
            total_re, total_im = complex_multiply(
                total_re, total_im, ratio_re[:, pick], ratio_im[:, pick]
            )
        return total_re[:, None, None], total_im[:, None, None]

    def scale(gain, values):
        moved = complex_multiply(gain[0], gain[1], values[:, 0:1], values[:, 1:2])
        return jnp.concatenate(moved, axis=1)

    table_rows = sine_rows(lax.optimization_barrier(jnp.arange(columns, dtype=jnp.int32)), columns)
    phase_re, phase_im = cayley_factor(columns, diffraction)
    along_y = cayley_rows(amplified, table_rows, phase_re, phase_im)

    edge_rows = jnp.array([0, block + 1], dtype=jnp.int32)
    edges = apply_block(
        green_re[:, edge_rows, 1 : block + 1], green_im[:, edge_rows, 1 : block + 1], along_y
    )
    from_left = shifted(edges[1], "gx", 1)
    from_right = shifted(edges[0], "gx", -1)
    span = 1
    while span < count - 1:
        far_left = shifted(from_left, "gx", span)
        far_right = shifted(from_right, "gx", -span)
        from_left = from_left + scale(span_product(rise_re, rise_im, me - span, span), far_left)
        from_right = from_right + scale(span_product(fall_re, fall_im, me + 1, span), far_right)
        span *= 2

    local = apply_block(
        green_re[:, 1 : block + 1, 1 : block + 1], green_im[:, 1 : block + 1, 1 : block + 1], along_y
    )
    lead_re, lead_im = safe_ratio(
        green_re[:, 1 : block + 1, 0],
        green_im[:, 1 : block + 1, 0],
        green_re[:, 1:2, 0],
        green_im[:, 1:2, 0],
    )
    trail_re, trail_im = safe_ratio(
        green_re[:, 1 : block + 1, block + 1],
        green_im[:, 1 : block + 1, block + 1],
        green_re[:, block : block + 1, block + 1],
        green_im[:, block : block + 1, block + 1],
    )
    lead = complex_multiply(
        lead_re.T[:, :, None], lead_im.T[:, :, None], from_left[None, :, 0], from_left[None, :, 1]
    )
    trail = complex_multiply(
        trail_re.T[:, :, None], trail_im.T[:, :, None], from_right[None, :, 0], from_right[None, :, 1]
    )
    solved = local + jnp.stack([lead[0] + trail[0], lead[1] + trail[1]], axis=2)
    result = 2.0 * solved - along_y

    fluence_out = butterfly_sum(power_sum(result), "wl")
    gain_out = base_gain / (1.0 + fluence_out / spectra)
    return (result * jnp.exp(0.5 * gain_out)[:, None, None, :], gain_out)


def solution(mesh):
    placed = (P("gx", "wl", None, None), P("gx", None), P(), P("wl"), P("wl"))
    return jax.shard_map(
        shards,
        mesh=mesh,
        in_specs=placed,
        out_specs=(P("gx", "wl", None, None), P("gx", None)),
        check_vma=False,
    )
```

```python
import math

import jax
import jax.numpy as jnp
from jax import lax
from jax.sharding import PartitionSpec as P

HIGHEST = lax.Precision.HIGHEST
HIGH = lax.Precision.HIGH


def complex_multiply(left_re, left_im, right_re, right_im):
    return (left_re * right_re - left_im * right_im, left_re * right_im + left_im * right_re)


def complex_div(top_re, top_im, bottom_re, bottom_im):
    magnitude = bottom_re * bottom_re + bottom_im * bottom_im
    return (
        (top_re * bottom_re + top_im * bottom_im) / magnitude,
        (top_im * bottom_re - top_re * bottom_im) / magnitude,
    )


def sine_rows(index, length):
    mode = jnp.arange(1, length + 1, dtype=jnp.int32)
    product = ((index + 1)[:, None] * mode[None, :]) % (2 * (length + 1))
    value = jnp.sin(product.astype(jnp.float32) * (math.pi / (length + 1))) * math.sqrt(
        2.0 / (length + 1)
    )
    inside = ((index >= 0) & (index < length))[:, None]
    return jnp.where(inside, value, 0.0)


def eigen_scaled(length, diffraction):
    counter = jnp.arange(1, length + 1, dtype=jnp.float32)
    eigenvalue = 4.0 * jnp.sin(counter * (math.pi / (2 * (length + 1)))) ** 2
    return diffraction[:, None] * eigenvalue[None, :]


def inverse_factor(length, diffraction):
    scaled = eigen_scaled(length, diffraction)
    magnitude = 1.0 + scaled * scaled
    return 1.0 / magnitude, -scaled / magnitude


def butterfly_sum(value, axis):
    count = lax.axis_size(axis)
    if count & (count - 1):
        return lax.psum(value, axis)
    step = 1
    while step < count:
        pairs = [(i, i ^ step) for i in range(count)]
        value = value + lax.ppermute(value, axis, pairs)
        step *= 2
    return value


def shifted(value, axis, offset):
    count = lax.axis_size(axis)
    pairs = [(i, i + offset) for i in range(count) if 0 <= i + offset < count]
    return jax.tree.map(lambda part: lax.ppermute(part, axis, pairs), value)


def green_entries(rows, cols, factor_re, factor_im, length):
    row_table = sine_rows(rows, length)
    col_table = sine_rows(cols, length)
    both = row_table * col_table
    return (
        jnp.einsum("mn,wn->wm", both, factor_re, precision=HIGHEST),
        jnp.einsum("mn,wn->wm", both, factor_im, precision=HIGHEST),
    )


def safe_ratio(top_re, top_im, bottom_re, bottom_im):
    empty = (bottom_re == 0.0) & (bottom_im == 0.0)
    ratio_re, ratio_im = complex_div(
        top_re, top_im, jnp.where(empty, 1.0, bottom_re), bottom_im
    )
    return jnp.where(empty, 0.0, ratio_re), jnp.where(empty, 0.0, ratio_im)


def mode_sines(rows, modes, length):
    product = ((rows + 1)[:, None] * modes[None, :]) % (2 * (length + 1))
    return jnp.sin(product.astype(jnp.float32) * (math.pi / (length + 1))) * math.sqrt(
        2.0 / (length + 1)
    )


def cayley_spectrum(modes, length, diffraction):
    eigenvalue = 4.0 * jnp.sin(modes.astype(jnp.float32) * (math.pi / (2 * (length + 1)))) ** 2
    scaled = diffraction[:, None] * eigenvalue[None, :]
    magnitude = 1.0 + scaled * scaled
    return (1.0 - scaled * scaled) / magnitude, -2.0 * scaled / magnitude


def phased(spectrum, phase_re, phase_im):
    mixed_re, mixed_im = complex_multiply(
        spectrum[..., 0, :], spectrum[..., 1, :], phase_re, phase_im
    )
    return jnp.stack([mixed_re, mixed_im], axis=-2)


def cayley_rows(values, diffraction):
    length = values.shape[-1]
    counter = lax.optimization_barrier(jnp.arange(length, dtype=jnp.int32))
    if length % 2:
        table = mode_sines(counter, counter + 1, length)
        phase = cayley_spectrum(counter + 1, length, diffraction)
        spectrum = jnp.dot(values, table, precision=HIGH)
        return jnp.dot(phased(spectrum, *phase), table, precision=HIGH)
    half = length // 2
    rows = counter[:half]
    odd_table = mode_sines(rows, 2 * rows + 1, length)
    even_table = mode_sines(rows, 2 * rows + 2, length)
    low = values[..., :half]
    high = jnp.flip(values[..., half:], -1)
    odd = jnp.dot(low + high, odd_table, precision=HIGH)
    even = jnp.dot(low - high, even_table, precision=HIGH)
    odd = phased(odd, *cayley_spectrum(2 * rows + 1, length, diffraction))
    even = phased(even, *cayley_spectrum(2 * rows + 2, length, diffraction))
    back_odd = jnp.einsum("...q,jq->...j", odd, odd_table, precision=HIGH)
    back_even = jnp.einsum("...q,jq->...j", even, even_table, precision=HIGH)
    return jnp.concatenate(
        [back_odd + back_even, jnp.flip(back_odd - back_even, -1)], axis=-1
    )


def shards(beam_field, region_labels, gain_table, diffraction, spectral_weight):
    block, spectra_dev, _, columns = beam_field.shape
    spectra = spectra_dev * lax.axis_size("wl")
    count = lax.axis_size("gx")
    me = lax.axis_index("gx")
    cells = block * count
    regions = gain_table.shape[0]
    region_index = jnp.arange(regions, dtype=jnp.int32)
    base_gain = jnp.sum(
        jnp.where(
            region_labels[None] == region_index[:, None, None], gain_table[:, None, None], 0.0
        ),
        axis=0,
    )

    def power_sum(values):
        return jnp.sum(spectral_weight[None, :, None, None] * (values * values), axis=(1, 2))

    fluence_in = butterfly_sum(power_sum(beam_field), "wl")
    gain_in = base_gain / (1.0 + fluence_in / spectra)
    amplified = beam_field * jnp.exp(0.5 * gain_in)[:, None, None, :]

    factor_re, factor_im = inverse_factor(cells, diffraction)
    start = me * block
    around = start - 1 + jnp.arange(block + 2, dtype=jnp.int32)
    around_table = sine_rows(around, cells)
    green_re = jnp.einsum(
        "an,wn,bn->wab", around_table, factor_re, around_table, precision=HIGHEST
    )
    green_im = jnp.einsum(
        "an,wn,bn->wab", around_table, factor_im, around_table, precision=HIGHEST
    )

    def apply_block(rows_re, rows_im, values):
        kernel = jnp.stack(
            [
                jnp.stack([rows_re, -rows_im], axis=2),
                jnp.stack([rows_im, rows_re], axis=2),
            ],
            axis=1,
        )
        return jnp.einsum("wdack,kwcy->awdy", kernel, values, precision=HIGHEST)

    block_index = jnp.arange(count, dtype=jnp.int32)
    starts = block_index * block
    ends = starts + block - 1
    rise_re, rise_im = safe_ratio(
        *green_entries(starts + block, starts - 1, factor_re, factor_im, cells),
        *green_entries(starts, starts - 1, factor_re, factor_im, cells),
    )
    fall_re, fall_im = safe_ratio(
        *green_entries(ends - block, ends + 1, factor_re, factor_im, cells),
        *green_entries(ends, ends + 1, factor_re, factor_im, cells),
    )

    def span_product(ratio_re, ratio_im, first, length):
        total_re = jnp.ones_like(ratio_re[:, 0])
        total_im = jnp.zeros_like(ratio_im[:, 0])
        for offset in range(length):
            pick = jnp.clip(first + offset, 0, count - 1)
            total_re, total_im = complex_multiply(
                total_re, total_im, ratio_re[:, pick], ratio_im[:, pick]
            )
        return total_re[:, None, None], total_im[:, None, None]

    def scale(gain, values):
        moved = complex_multiply(gain[0], gain[1], values[:, 0:1], values[:, 1:2])
        return jnp.concatenate(moved, axis=1)

    along_y = cayley_rows(amplified, diffraction)

    edge_rows = jnp.array([0, block + 1], dtype=jnp.int32)
    edges = apply_block(
        green_re[:, edge_rows, 1 : block + 1], green_im[:, edge_rows, 1 : block + 1], along_y
    )
    from_left = shifted(edges[1], "gx", 1)
    from_right = shifted(edges[0], "gx", -1)
    span = 1
    while span < count - 1:
        far_left = shifted(from_left, "gx", span)
        far_right = shifted(from_right, "gx", -span)
        from_left = from_left + scale(span_product(rise_re, rise_im, me - span, span), far_left)
        from_right = from_right + scale(span_product(fall_re, fall_im, me + 1, span), far_right)
        span *= 2

    local = apply_block(
        green_re[:, 1 : block + 1, 1 : block + 1], green_im[:, 1 : block + 1, 1 : block + 1], along_y
    )
    lead_re, lead_im = safe_ratio(
        green_re[:, 1 : block + 1, 0],
        green_im[:, 1 : block + 1, 0],
        green_re[:, 1:2, 0],
        green_im[:, 1:2, 0],
    )
    trail_re, trail_im = safe_ratio(
        green_re[:, 1 : block + 1, block + 1],
        green_im[:, 1 : block + 1, block + 1],
        green_re[:, block : block + 1, block + 1],
        green_im[:, block : block + 1, block + 1],
    )
    lead = complex_multiply(
        lead_re.T[:, :, None], lead_im.T[:, :, None], from_left[None, :, 0], from_left[None, :, 1]
    )
    trail = complex_multiply(
        trail_re.T[:, :, None], trail_im.T[:, :, None], from_right[None, :, 0], from_right[None, :, 1]
    )
    solved = local + jnp.stack([lead[0] + trail[0], lead[1] + trail[1]], axis=2)
    result = 2.0 * solved - along_y

    fluence_out = butterfly_sum(power_sum(result), "wl")
    gain_out = base_gain / (1.0 + fluence_out / spectra)
    return (result * jnp.exp(0.5 * gain_out)[:, None, None, :], gain_out)


def solution(mesh):
    placed = (P("gx", "wl", None, None), P("gx", None), P(), P("wl"), P("wl"))
    return jax.shard_map(
        shards,
        mesh=mesh,
        in_specs=placed,
        out_specs=(P("gx", "wl", None, None), P("gx", None)),
        check_vma=False,
    )
```

```python
import math

import jax
import jax.numpy as jnp
from jax import lax
from jax.sharding import PartitionSpec as P

HIGHEST = lax.Precision.HIGHEST
HIGH = lax.Precision.HIGH


def complex_multiply(left_re, left_im, right_re, right_im):
    return (left_re * right_re - left_im * right_im, left_re * right_im + left_im * right_re)


def complex_div(top_re, top_im, bottom_re, bottom_im):
    magnitude = bottom_re * bottom_re + bottom_im * bottom_im
    return (
        (top_re * bottom_re + top_im * bottom_im) / magnitude,
        (top_im * bottom_re - top_re * bottom_im) / magnitude,
    )


def sine_rows(index, length):
    mode = jnp.arange(1, length + 1, dtype=jnp.int32)
    product = ((index + 1)[:, None] * mode[None, :]) % (2 * (length + 1))
    value = jnp.sin(product.astype(jnp.float32) * (math.pi / (length + 1))) * math.sqrt(
        2.0 / (length + 1)
    )
    inside = ((index >= 0) & (index < length))[:, None]
    return jnp.where(inside, value, 0.0)


def eigen_scaled(length, diffraction):
    counter = jnp.arange(1, length + 1, dtype=jnp.float32)
    eigenvalue = 4.0 * jnp.sin(counter * (math.pi / (2 * (length + 1)))) ** 2
    return diffraction[:, None] * eigenvalue[None, :]


def inverse_factor(length, diffraction):
    scaled = eigen_scaled(length, diffraction)
    magnitude = 1.0 + scaled * scaled
    return 1.0 / magnitude, -scaled / magnitude


def butterfly_sum(value, axis):
    count = lax.axis_size(axis)
    if count & (count - 1):
        return lax.psum(value, axis)
    step = 1
    while step < count:
        pairs = [(i, i ^ step) for i in range(count)]
        value = value + lax.ppermute(value, axis, pairs)
        step *= 2
    return value


def shifted(value, axis, offset):
    count = lax.axis_size(axis)
    pairs = [(i, i + offset) for i in range(count) if 0 <= i + offset < count]
    return jax.tree.map(lambda part: lax.ppermute(part, axis, pairs), value)


def green_entries(rows, cols, factor_re, factor_im, length):
    row_table = sine_rows(rows, length)
    col_table = sine_rows(cols, length)
    both = row_table * col_table
    return (
        jnp.einsum("mn,wn->wm", both, factor_re, precision=HIGHEST),
        jnp.einsum("mn,wn->wm", both, factor_im, precision=HIGHEST),
    )


def safe_ratio(top_re, top_im, bottom_re, bottom_im):
    empty = (bottom_re == 0.0) & (bottom_im == 0.0)
    ratio_re, ratio_im = complex_div(
        top_re, top_im, jnp.where(empty, 1.0, bottom_re), bottom_im
    )
    return jnp.where(empty, 0.0, ratio_re), jnp.where(empty, 0.0, ratio_im)


def mode_sines(rows, modes, length):
    product = ((rows + 1)[:, None] * modes[None, :]) % (2 * (length + 1))
    return jnp.sin(product.astype(jnp.float32) * (math.pi / (length + 1))) * math.sqrt(
        2.0 / (length + 1)
    )


def cayley_spectrum(modes, length, diffraction):
    eigenvalue = 4.0 * jnp.sin(modes.astype(jnp.float32) * (math.pi / (2 * (length + 1)))) ** 2
    scaled = diffraction[:, None] * eigenvalue[None, :]
    magnitude = 1.0 + scaled * scaled
    return (1.0 - scaled * scaled) / magnitude, -2.0 * scaled / magnitude


def phased(spectrum, phase_re, phase_im):
    mixed_re, mixed_im = complex_multiply(
        spectrum[..., 0, :, :], spectrum[..., 1, :, :], phase_re, phase_im
    )
    return jnp.stack([mixed_re, mixed_im], axis=-3)


def cayley_rows(values, diffraction):
    length = values.shape[-1]
    counter = lax.optimization_barrier(jnp.arange(length, dtype=jnp.int32))
    if length % 2:
        table = mode_sines(counter, counter + 1, length)
        phase = cayley_spectrum(counter + 1, length, diffraction)
        spectrum = jnp.dot(values, table, precision=HIGH)
        return jnp.dot(phased(spectrum, *phase), table, precision=HIGH)
    half = length // 2
    rows = counter[:half]
    odd_table = mode_sines(rows, 2 * rows + 1, length)
    even_table = mode_sines(rows, 2 * rows + 2, length)
    low = values[..., :half]
    high = jnp.flip(values[..., half:], -1)
    odd = jnp.dot(low + high, odd_table, precision=HIGH)
    even = jnp.dot(low - high, even_table, precision=HIGH)
    odd = phased(odd, *cayley_spectrum(2 * rows + 1, length, diffraction))
    even = phased(even, *cayley_spectrum(2 * rows + 2, length, diffraction))
    back_odd = jnp.einsum("...q,jq->...j", odd, odd_table, precision=HIGH)
    back_even = jnp.einsum("...q,jq->...j", even, even_table, precision=HIGH)
    return jnp.concatenate(
        [back_odd + back_even, jnp.flip(back_odd - back_even, -1)], axis=-1
    )


def shards(beam_field, region_labels, gain_table, diffraction, spectral_weight):
    block, spectra_dev, _, columns = beam_field.shape
    spectra = spectra_dev * lax.axis_size("wl")
    count = lax.axis_size("gx")
    me = lax.axis_index("gx")
    cells = block * count
    regions = gain_table.shape[0]
    region_index = jnp.arange(regions, dtype=jnp.int32)
    base_gain = jnp.sum(
        jnp.where(
            region_labels[None] == region_index[:, None, None], gain_table[:, None, None], 0.0
        ),
        axis=0,
    )

    def power_sum(values):
        return jnp.sum(spectral_weight[None, :, None, None] * (values * values), axis=(1, 2))

    fluence_in = butterfly_sum(power_sum(beam_field), "wl")
    gain_in = base_gain / (1.0 + fluence_in / spectra)
    amplified = jnp.transpose(beam_field, (0, 2, 1, 3)) * jnp.exp(0.5 * gain_in)[:, None, None, :]

    factor_re, factor_im = inverse_factor(cells, diffraction)
    start = me * block
    around = start - 1 + jnp.arange(block + 2, dtype=jnp.int32)
    around_table = sine_rows(around, cells)
    green_re = jnp.einsum(
        "an,wn,bn->wab", around_table, factor_re, around_table, precision=HIGHEST
    )
    green_im = jnp.einsum(
        "an,wn,bn->wab", around_table, factor_im, around_table, precision=HIGHEST
    )

    def apply_block(rows_re, rows_im, values):
        kernel = jnp.stack(
            [
                jnp.stack([rows_re, -rows_im], axis=2),
                jnp.stack([rows_im, rows_re], axis=2),
            ],
            axis=1,
        )
        return jnp.einsum("wdack,kcwy->adwy", kernel, values, precision=HIGH)

    block_index = jnp.arange(count, dtype=jnp.int32)
    starts = block_index * block
    ends = starts + block - 1
    rise_re, rise_im = safe_ratio(
        *green_entries(starts + block, starts - 1, factor_re, factor_im, cells),
        *green_entries(starts, starts - 1, factor_re, factor_im, cells),
    )
    fall_re, fall_im = safe_ratio(
        *green_entries(ends - block, ends + 1, factor_re, factor_im, cells),
        *green_entries(ends, ends + 1, factor_re, factor_im, cells),
    )

    def span_product(ratio_re, ratio_im, first, length):
        total_re = jnp.ones_like(ratio_re[:, 0])
        total_im = jnp.zeros_like(ratio_im[:, 0])
        for offset in range(length):
            pick = jnp.clip(first + offset, 0, count - 1)
            total_re, total_im = complex_multiply(
                total_re, total_im, ratio_re[:, pick], ratio_im[:, pick]
            )
        return total_re[None, :, None], total_im[None, :, None]

    def scale(gain, values):
        moved = complex_multiply(gain[0], gain[1], values[0:1], values[1:2])
        return jnp.concatenate(moved, axis=0)

    along_y = cayley_rows(amplified, diffraction)

    edge_rows = jnp.array([0, block + 1], dtype=jnp.int32)
    edges = apply_block(
        green_re[:, edge_rows, 1 : block + 1], green_im[:, edge_rows, 1 : block + 1], along_y
    )
    from_left = shifted(edges[1], "gx", 1)
    from_right = shifted(edges[0], "gx", -1)
    span = 1
    while span < count - 1:
        far_left = shifted(from_left, "gx", span)
        far_right = shifted(from_right, "gx", -span)
        from_left = from_left + scale(span_product(rise_re, rise_im, me - span, span), far_left)
        from_right = from_right + scale(span_product(fall_re, fall_im, me + 1, span), far_right)
        span *= 2

    local = apply_block(
        green_re[:, 1 : block + 1, 1 : block + 1], green_im[:, 1 : block + 1, 1 : block + 1], along_y
    )
    lead_re, lead_im = safe_ratio(
        green_re[:, 1 : block + 1, 0],
        green_im[:, 1 : block + 1, 0],
        green_re[:, 1:2, 0],
        green_im[:, 1:2, 0],
    )
    trail_re, trail_im = safe_ratio(
        green_re[:, 1 : block + 1, block + 1],
        green_im[:, 1 : block + 1, block + 1],
        green_re[:, block : block + 1, block + 1],
        green_im[:, block : block + 1, block + 1],
    )
    lead = complex_multiply(
        lead_re.T[:, :, None], lead_im.T[:, :, None], from_left[None, 0], from_left[None, 1]
    )
    trail = complex_multiply(
        trail_re.T[:, :, None], trail_im.T[:, :, None], from_right[None, 0], from_right[None, 1]
    )
    solved = local + jnp.stack([lead[0] + trail[0], lead[1] + trail[1]], axis=1)
    result = jnp.transpose(2.0 * solved - along_y, (0, 2, 1, 3))

    fluence_out = butterfly_sum(power_sum(result), "wl")
    gain_out = base_gain / (1.0 + fluence_out / spectra)
    return (result * jnp.exp(0.5 * gain_out)[:, None, None, :], gain_out)


def solution(mesh):
    placed = (P("gx", "wl", None, None), P("gx", None), P(), P("wl"), P("wl"))
    return jax.shard_map(
        shards,
        mesh=mesh,
        in_specs=placed,
        out_specs=(P("gx", "wl", None, None), P("gx", None)),
        check_vma=False,
    )
```

```python
import math

import jax
import jax.numpy as jnp
from jax import lax
from jax.experimental.layout import Layout, with_layout_constraint
from jax.sharding import PartitionSpec as P

HIGHEST = lax.Precision.HIGHEST
HIGH = lax.Precision.HIGH


def complex_multiply(left_re, left_im, right_re, right_im):
    return (left_re * right_re - left_im * right_im, left_re * right_im + left_im * right_re)


def complex_div(top_re, top_im, bottom_re, bottom_im):
    magnitude = bottom_re * bottom_re + bottom_im * bottom_im
    return (
        (top_re * bottom_re + top_im * bottom_im) / magnitude,
        (top_im * bottom_re - top_re * bottom_im) / magnitude,
    )


def sine_rows(index, length):
    mode = jnp.arange(1, length + 1, dtype=jnp.int32)
    product = ((index + 1)[:, None] * mode[None, :]) % (2 * (length + 1))
    value = jnp.sin(product.astype(jnp.float32) * (math.pi / (length + 1))) * math.sqrt(
        2.0 / (length + 1)
    )
    inside = ((index >= 0) & (index < length))[:, None]
    return jnp.where(inside, value, 0.0)


def eigen_scaled(length, diffraction):
    counter = jnp.arange(1, length + 1, dtype=jnp.float32)
    eigenvalue = 4.0 * jnp.sin(counter * (math.pi / (2 * (length + 1)))) ** 2
    return diffraction[:, None] * eigenvalue[None, :]


def inverse_factor(length, diffraction):
    scaled = eigen_scaled(length, diffraction)
    magnitude = 1.0 + scaled * scaled
    return 1.0 / magnitude, -scaled / magnitude


def butterfly_sum(value, axis):
    count = lax.axis_size(axis)
    if count & (count - 1):
        return lax.psum(value, axis)
    step = 1
    while step < count:
        pairs = [(i, i ^ step) for i in range(count)]
        value = value + lax.ppermute(value, axis, pairs)
        step *= 2
    return value


def shifted(value, axis, offset):
    count = lax.axis_size(axis)
    pairs = [(i, i + offset) for i in range(count) if 0 <= i + offset < count]
    return jax.tree.map(lambda part: lax.ppermute(part, axis, pairs), value)


def green_entries(rows, cols, factor_re, factor_im, length):
    row_table = sine_rows(rows, length)
    col_table = sine_rows(cols, length)
    both = row_table * col_table
    return (
        jnp.einsum("mn,wn->wm", both, factor_re, precision=HIGHEST),
        jnp.einsum("mn,wn->wm", both, factor_im, precision=HIGHEST),
    )


def safe_ratio(top_re, top_im, bottom_re, bottom_im):
    empty = (bottom_re == 0.0) & (bottom_im == 0.0)
    ratio_re, ratio_im = complex_div(
        top_re, top_im, jnp.where(empty, 1.0, bottom_re), bottom_im
    )
    return jnp.where(empty, 0.0, ratio_re), jnp.where(empty, 0.0, ratio_im)


def mode_sines(rows, modes, length):
    product = ((rows + 1)[:, None] * modes[None, :]) % (2 * (length + 1))
    return jnp.sin(product.astype(jnp.float32) * (math.pi / (length + 1))) * math.sqrt(
        2.0 / (length + 1)
    )


def cayley_spectrum(modes, length, diffraction):
    eigenvalue = 4.0 * jnp.sin(modes.astype(jnp.float32) * (math.pi / (2 * (length + 1)))) ** 2
    scaled = diffraction[:, None] * eigenvalue[None, :]
    magnitude = 1.0 + scaled * scaled
    return (1.0 - scaled * scaled) / magnitude, -2.0 * scaled / magnitude


def phased(spectrum, phase_re, phase_im):
    mixed_re, mixed_im = complex_multiply(
        spectrum[..., 0, :, :], spectrum[..., 1, :, :], phase_re, phase_im
    )
    return jnp.stack([mixed_re, mixed_im], axis=-3)


def cayley_rows(values, diffraction):
    length = values.shape[-1]
    counter = lax.optimization_barrier(jnp.arange(length, dtype=jnp.int32))
    if length % 2:
        table = mode_sines(counter, counter + 1, length)
        phase = cayley_spectrum(counter + 1, length, diffraction)
        spectrum = jnp.dot(values, table, precision=HIGH)
        return jnp.dot(phased(spectrum, *phase), table, precision=HIGH)
    half = length // 2
    rows = counter[:half]
    odd_table = mode_sines(rows, 2 * rows + 1, length)
    even_table = mode_sines(rows, 2 * rows + 2, length)
    low = values[..., :half]
    high = jnp.flip(values[..., half:], -1)
    odd = jnp.dot(low + high, odd_table, precision=HIGH)
    even = jnp.dot(low - high, even_table, precision=HIGH)
    odd = phased(odd, *cayley_spectrum(2 * rows + 1, length, diffraction))
    even = phased(even, *cayley_spectrum(2 * rows + 2, length, diffraction))
    back_odd = jnp.einsum("...q,jq->...j", odd, odd_table, precision=HIGH)
    back_even = jnp.einsum("...q,jq->...j", even, even_table, precision=HIGH)
    return jnp.concatenate(
        [back_odd + back_even, jnp.flip(back_odd - back_even, -1)], axis=-1
    )


def shards(beam_field, region_labels, gain_table, diffraction, spectral_weight):
    block, spectra_dev, _, columns = beam_field.shape
    spectra = spectra_dev * lax.axis_size("wl")
    count = lax.axis_size("gx")
    me = lax.axis_index("gx")
    cells = block * count
    regions = gain_table.shape[0]
    region_index = jnp.arange(regions, dtype=jnp.int32)
    base_gain = jnp.sum(
        jnp.where(
            region_labels[None] == region_index[:, None, None], gain_table[:, None, None], 0.0
        ),
        axis=0,
    )

    def power_sum(values):
        return jnp.sum(spectral_weight[None, :, None, None] * (values * values), axis=(1, 2))

    fluence_in = butterfly_sum(power_sum(beam_field), "wl")
    gain_in = base_gain / (1.0 + fluence_in / spectra)
    amplified = with_layout_constraint(
        jnp.transpose(beam_field, (0, 2, 1, 3)) * jnp.exp(0.5 * gain_in)[:, None, None, :],
        Layout(major_to_minor=(0, 1, 2, 3)),
    )

    factor_re, factor_im = inverse_factor(cells, diffraction)
    start = me * block
    around = start - 1 + jnp.arange(block + 2, dtype=jnp.int32)
    around_table = sine_rows(around, cells)
    green_re = jnp.einsum(
        "an,wn,bn->wab", around_table, factor_re, around_table, precision=HIGHEST
    )
    green_im = jnp.einsum(
        "an,wn,bn->wab", around_table, factor_im, around_table, precision=HIGHEST
    )

    def apply_block(rows_re, rows_im, values):
        kernel = jnp.stack(
            [
                jnp.stack([rows_re, -rows_im], axis=2),
                jnp.stack([rows_im, rows_re], axis=2),
            ],
            axis=1,
        )
        return jnp.einsum("wdack,kcwy->adwy", kernel, values, precision=HIGH)

    block_index = jnp.arange(count, dtype=jnp.int32)
    starts = block_index * block
    ends = starts + block - 1
    rise_re, rise_im = safe_ratio(
        *green_entries(starts + block, starts - 1, factor_re, factor_im, cells),
        *green_entries(starts, starts - 1, factor_re, factor_im, cells),
    )
    fall_re, fall_im = safe_ratio(
        *green_entries(ends - block, ends + 1, factor_re, factor_im, cells),
        *green_entries(ends, ends + 1, factor_re, factor_im, cells),
    )

    def span_product(ratio_re, ratio_im, first, length):
        total_re = jnp.ones_like(ratio_re[:, 0])
        total_im = jnp.zeros_like(ratio_im[:, 0])
        for offset in range(length):
            pick = jnp.clip(first + offset, 0, count - 1)
            total_re, total_im = complex_multiply(
                total_re, total_im, ratio_re[:, pick], ratio_im[:, pick]
            )
        return total_re[None, :, None], total_im[None, :, None]

    def scale(gain, values):
        moved = complex_multiply(gain[0], gain[1], values[0:1], values[1:2])
        return jnp.concatenate(moved, axis=0)

    along_y = cayley_rows(amplified, diffraction)

    edge_rows = jnp.array([0, block + 1], dtype=jnp.int32)
    edges = apply_block(
        green_re[:, edge_rows, 1 : block + 1], green_im[:, edge_rows, 1 : block + 1], along_y
    )
    from_left = shifted(edges[1], "gx", 1)
    from_right = shifted(edges[0], "gx", -1)
    span = 1
    while span < count - 1:
        far_left = shifted(from_left, "gx", span)
        far_right = shifted(from_right, "gx", -span)
        from_left = from_left + scale(span_product(rise_re, rise_im, me - span, span), far_left)
        from_right = from_right + scale(span_product(fall_re, fall_im, me + 1, span), far_right)
        span *= 2

    local = apply_block(
        green_re[:, 1 : block + 1, 1 : block + 1], green_im[:, 1 : block + 1, 1 : block + 1], along_y
    )
    lead_re, lead_im = safe_ratio(
        green_re[:, 1 : block + 1, 0],
        green_im[:, 1 : block + 1, 0],
        green_re[:, 1:2, 0],
        green_im[:, 1:2, 0],
    )
    trail_re, trail_im = safe_ratio(
        green_re[:, 1 : block + 1, block + 1],
        green_im[:, 1 : block + 1, block + 1],
        green_re[:, block : block + 1, block + 1],
        green_im[:, block : block + 1, block + 1],
    )
    lead = complex_multiply(
        lead_re.T[:, :, None], lead_im.T[:, :, None], from_left[None, 0], from_left[None, 1]
    )
    trail = complex_multiply(
        trail_re.T[:, :, None], trail_im.T[:, :, None], from_right[None, 0], from_right[None, 1]
    )
    solved = local + jnp.stack([lead[0] + trail[0], lead[1] + trail[1]], axis=1)
    result = jnp.transpose(2.0 * solved - along_y, (0, 2, 1, 3))

    fluence_out = butterfly_sum(power_sum(result), "wl")
    gain_out = base_gain / (1.0 + fluence_out / spectra)
    return (result * jnp.exp(0.5 * gain_out)[:, None, None, :], gain_out)


def solution(mesh):
    placed = (P("gx", "wl", None, None), P("gx", None), P(), P("wl"), P("wl"))
    return jax.shard_map(
        shards,
        mesh=mesh,
        in_specs=placed,
        out_specs=(P("gx", "wl", None, None), P("gx", None)),
        check_vma=False,
    )
```

```python
import math

import jax
import jax.numpy as jnp
from jax import lax
from jax.experimental.layout import Layout, with_layout_constraint
from jax.sharding import PartitionSpec as P

HIGHEST = lax.Precision.HIGHEST
HIGH = lax.Precision.HIGH


def complex_multiply(left_re, left_im, right_re, right_im):
    return (left_re * right_re - left_im * right_im, left_re * right_im + left_im * right_re)


def complex_div(top_re, top_im, bottom_re, bottom_im):
    magnitude = bottom_re * bottom_re + bottom_im * bottom_im
    return (
        (top_re * bottom_re + top_im * bottom_im) / magnitude,
        (top_im * bottom_re - top_re * bottom_im) / magnitude,
    )


def sine_rows(index, length):
    mode = jnp.arange(1, length + 1, dtype=jnp.int32)
    product = ((index + 1)[:, None] * mode[None, :]) % (2 * (length + 1))
    value = jnp.sin(product.astype(jnp.float32) * (math.pi / (length + 1))) * math.sqrt(
        2.0 / (length + 1)
    )
    inside = ((index >= 0) & (index < length))[:, None]
    return jnp.where(inside, value, 0.0)


def eigen_scaled(length, diffraction):
    counter = jnp.arange(1, length + 1, dtype=jnp.float32)
    eigenvalue = 4.0 * jnp.sin(counter * (math.pi / (2 * (length + 1)))) ** 2
    return diffraction[:, None] * eigenvalue[None, :]


def inverse_factor(length, diffraction):
    scaled = eigen_scaled(length, diffraction)
    magnitude = 1.0 + scaled * scaled
    return 1.0 / magnitude, -scaled / magnitude


def butterfly_sum(value, axis):
    count = lax.axis_size(axis)
    if count & (count - 1):
        return lax.psum(value, axis)
    step = 1
    while step < count:
        pairs = [(i, i ^ step) for i in range(count)]
        value = value + lax.ppermute(value, axis, pairs)
        step *= 2
    return value


def shifted(value, axis, offset):
    count = lax.axis_size(axis)
    pairs = [(i, i + offset) for i in range(count) if 0 <= i + offset < count]
    return jax.tree.map(lambda part: lax.ppermute(part, axis, pairs), value)


def green_entries(rows, cols, factor_re, factor_im, length):
    row_table = sine_rows(rows, length)
    col_table = sine_rows(cols, length)
    both = row_table * col_table
    return (
        jnp.einsum("mn,wn->wm", both, factor_re, precision=HIGHEST),
        jnp.einsum("mn,wn->wm", both, factor_im, precision=HIGHEST),
    )


def safe_ratio(top_re, top_im, bottom_re, bottom_im):
    empty = (bottom_re == 0.0) & (bottom_im == 0.0)
    ratio_re, ratio_im = complex_div(
        top_re, top_im, jnp.where(empty, 1.0, bottom_re), bottom_im
    )
    return jnp.where(empty, 0.0, ratio_re), jnp.where(empty, 0.0, ratio_im)


def mode_sines(rows, modes, length):
    product = ((rows + 1)[:, None] * modes[None, :]) % (2 * (length + 1))
    return jnp.sin(product.astype(jnp.float32) * (math.pi / (length + 1))) * math.sqrt(
        2.0 / (length + 1)
    )


def cayley_spectrum(modes, length, diffraction):
    eigenvalue = 4.0 * jnp.sin(modes.astype(jnp.float32) * (math.pi / (2 * (length + 1)))) ** 2
    scaled = diffraction[:, None] * eigenvalue[None, :]
    magnitude = 1.0 + scaled * scaled
    return (1.0 - scaled * scaled) / magnitude, -2.0 * scaled / magnitude


def phased(spectrum, phase_re, phase_im):
    mixed_re, mixed_im = complex_multiply(
        spectrum[..., 0, :, :], spectrum[..., 1, :, :], phase_re, phase_im
    )
    return jnp.stack([mixed_re, mixed_im], axis=-3)


def cayley_rows(values, diffraction):
    length = values.shape[-1]
    counter = lax.optimization_barrier(jnp.arange(length, dtype=jnp.int32))
    if length % 2:
        table = mode_sines(counter, counter + 1, length)
        phase = cayley_spectrum(counter + 1, length, diffraction)
        spectrum = jnp.dot(values, table, precision=HIGH)
        return jnp.dot(phased(spectrum, *phase), table, precision=HIGH)
    half = length // 2
    rows = counter[:half]
    odd_table = mode_sines(rows, 2 * rows + 1, length)
    even_table = mode_sines(rows, 2 * rows + 2, length)
    low = values[..., :half]
    high = jnp.flip(values[..., half:], -1)
    odd = jnp.dot(low + high, odd_table, precision=HIGH)
    even = jnp.dot(low - high, even_table, precision=HIGH)
    odd = phased(odd, *cayley_spectrum(2 * rows + 1, length, diffraction))
    even = phased(even, *cayley_spectrum(2 * rows + 2, length, diffraction))
    back_odd = jnp.einsum("...q,jq->...j", odd, odd_table, precision=HIGH)
    back_even = jnp.einsum("...q,jq->...j", even, even_table, precision=HIGH)
    return jnp.concatenate(
        [back_odd + back_even, jnp.flip(back_odd - back_even, -1)], axis=-1
    )


def shards(beam_field, region_labels, gain_table, diffraction, spectral_weight):
    block, spectra_dev, _, columns = beam_field.shape
    spectra = spectra_dev * lax.axis_size("wl")
    count = lax.axis_size("gx")
    me = lax.axis_index("gx")
    cells = block * count
    regions = gain_table.shape[0]
    region_index = jnp.arange(regions, dtype=jnp.int32)
    base_gain = jnp.sum(
        jnp.where(
            region_labels[None] == region_index[:, None, None], gain_table[:, None, None], 0.0
        ),
        axis=0,
    )

    def power_sum(values):
        return jnp.sum(spectral_weight[None, :, None, None] * (values * values), axis=(1, 2))

    fluence_in = butterfly_sum(power_sum(beam_field), "wl")
    gain_in = base_gain / (1.0 + fluence_in / spectra)
    amplified = with_layout_constraint(
        jnp.transpose(beam_field, (0, 2, 1, 3)) * jnp.exp(0.5 * gain_in)[:, None, None, :],
        Layout(major_to_minor=(0, 1, 2, 3)),
    )

    factor_re, factor_im = inverse_factor(cells, diffraction)
    start = me * block
    around = start - 1 + jnp.arange(block + 2, dtype=jnp.int32)
    around_table = sine_rows(around, cells)
    green_re = jnp.einsum(
        "an,wn,bn->wab", around_table, factor_re, around_table, precision=HIGHEST
    )
    green_im = jnp.einsum(
        "an,wn,bn->wab", around_table, factor_im, around_table, precision=HIGHEST
    )

    def apply_block(rows_re, rows_im, values):
        kernel = jnp.stack(
            [
                jnp.stack([rows_re, -rows_im], axis=2),
                jnp.stack([rows_im, rows_re], axis=2),
            ],
            axis=1,
        )
        return jnp.einsum("wdack,kcwy->adwy", kernel, values, precision=HIGH)

    block_index = jnp.arange(count, dtype=jnp.int32)
    starts = block_index * block
    ends = starts + block - 1
    rise_re, rise_im = safe_ratio(
        *green_entries(starts + block, starts - 1, factor_re, factor_im, cells),
        *green_entries(starts, starts - 1, factor_re, factor_im, cells),
    )
    fall_re, fall_im = safe_ratio(
        *green_entries(ends - block, ends + 1, factor_re, factor_im, cells),
        *green_entries(ends, ends + 1, factor_re, factor_im, cells),
    )

    def span_product(ratio_re, ratio_im, first, length):
        total_re = jnp.ones_like(ratio_re[:, 0])
        total_im = jnp.zeros_like(ratio_im[:, 0])
        for offset in range(length):
            pick = jnp.clip(first + offset, 0, count - 1)
            total_re, total_im = complex_multiply(
                total_re, total_im, ratio_re[:, pick], ratio_im[:, pick]
            )
        return total_re[None, :, None], total_im[None, :, None]

    def scale(gain, values):
        moved = complex_multiply(gain[0], gain[1], values[0:1], values[1:2])
        return jnp.concatenate(moved, axis=0)

    along_y = cayley_rows(amplified, diffraction)

    edge_rows = jnp.array([0, block + 1], dtype=jnp.int32)
    edges = apply_block(
        green_re[:, edge_rows, 1 : block + 1], green_im[:, edge_rows, 1 : block + 1], along_y
    )
    if count <= 8:
        from_left = jnp.zeros_like(edges[1])
        from_right = jnp.zeros_like(edges[0])
        for span in range(1, count):
            far_left = shifted(edges[1], "gx", span)
            far_right = shifted(edges[0], "gx", -span)
            from_left = from_left + scale(
                span_product(rise_re, rise_im, me - span + 1, span - 1), far_left
            )
            from_right = from_right + scale(
                span_product(fall_re, fall_im, me + 1, span - 1), far_right
            )
        span = count
    else:
        from_left = shifted(edges[1], "gx", 1)
        from_right = shifted(edges[0], "gx", -1)
        span = 1
    while span < count - 1:
        far_left = shifted(from_left, "gx", span)
        far_right = shifted(from_right, "gx", -span)
        from_left = from_left + scale(span_product(rise_re, rise_im, me - span, span), far_left)
        from_right = from_right + scale(span_product(fall_re, fall_im, me + 1, span), far_right)
        span *= 2

    local = apply_block(
        green_re[:, 1 : block + 1, 1 : block + 1], green_im[:, 1 : block + 1, 1 : block + 1], along_y
    )
    lead_re, lead_im = safe_ratio(
        green_re[:, 1 : block + 1, 0],
        green_im[:, 1 : block + 1, 0],
        green_re[:, 1:2, 0],
        green_im[:, 1:2, 0],
    )
    trail_re, trail_im = safe_ratio(
        green_re[:, 1 : block + 1, block + 1],
        green_im[:, 1 : block + 1, block + 1],
        green_re[:, block : block + 1, block + 1],
        green_im[:, block : block + 1, block + 1],
    )
    lead = complex_multiply(
        lead_re.T[:, :, None], lead_im.T[:, :, None], from_left[None, 0], from_left[None, 1]
    )
    trail = complex_multiply(
        trail_re.T[:, :, None], trail_im.T[:, :, None], from_right[None, 0], from_right[None, 1]
    )
    solved = local + jnp.stack([lead[0] + trail[0], lead[1] + trail[1]], axis=1)
    result = jnp.transpose(2.0 * solved - along_y, (0, 2, 1, 3))

    fluence_out = butterfly_sum(power_sum(result), "wl")
    gain_out = base_gain / (1.0 + fluence_out / spectra)
    return (result * jnp.exp(0.5 * gain_out)[:, None, None, :], gain_out)


def solution(mesh):
    placed = (P("gx", "wl", None, None), P("gx", None), P(), P("wl"), P("wl"))
    return jax.shard_map(
        shards,
        mesh=mesh,
        in_specs=placed,
        out_specs=(P("gx", "wl", None, None), P("gx", None)),
        check_vma=False,
    )
```

```python
import math

import jax
import jax.numpy as jnp
from jax import lax
from jax.experimental.layout import Layout, with_layout_constraint
from jax.sharding import PartitionSpec as P

HIGHEST = lax.Precision.HIGHEST
HIGH = lax.Precision.HIGH


def complex_multiply(left_re, left_im, right_re, right_im):
    return (left_re * right_re - left_im * right_im, left_re * right_im + left_im * right_re)


def complex_div(top_re, top_im, bottom_re, bottom_im):
    magnitude = bottom_re * bottom_re + bottom_im * bottom_im
    return (
        (top_re * bottom_re + top_im * bottom_im) / magnitude,
        (top_im * bottom_re - top_re * bottom_im) / magnitude,
    )


def sine_rows(index, length):
    mode = jnp.arange(1, length + 1, dtype=jnp.int32)
    product = ((index + 1)[:, None] * mode[None, :]) % (2 * (length + 1))
    value = jnp.sin(product.astype(jnp.float32) * (math.pi / (length + 1))) * math.sqrt(
        2.0 / (length + 1)
    )
    inside = ((index >= 0) & (index < length))[:, None]
    return jnp.where(inside, value, 0.0)


def eigen_scaled(length, diffraction):
    counter = jnp.arange(1, length + 1, dtype=jnp.float32)
    eigenvalue = 4.0 * jnp.sin(counter * (math.pi / (2 * (length + 1)))) ** 2
    return diffraction[:, None] * eigenvalue[None, :]


def inverse_factor(length, diffraction):
    scaled = eigen_scaled(length, diffraction)
    magnitude = 1.0 + scaled * scaled
    return 1.0 / magnitude, -scaled / magnitude


def butterfly_sum(value, axis):
    count = lax.axis_size(axis)
    if count & (count - 1):
        return lax.psum(value, axis)
    step = 1
    while step < count:
        pairs = [(i, i ^ step) for i in range(count)]
        value = value + lax.ppermute(value, axis, pairs)
        step *= 2
    return value


def shifted(value, axis, offset):
    count = lax.axis_size(axis)
    pairs = [(i, i + offset) for i in range(count) if 0 <= i + offset < count]
    return jax.tree.map(lambda part: lax.ppermute(part, axis, pairs), value)


def green_entries(rows, cols, factor_re, factor_im, length):
    row_table = sine_rows(rows, length)
    col_table = sine_rows(cols, length)
    both = row_table * col_table
    return (
        jnp.einsum("mn,wn->wm", both, factor_re, precision=HIGHEST),
        jnp.einsum("mn,wn->wm", both, factor_im, precision=HIGHEST),
    )


def safe_ratio(top_re, top_im, bottom_re, bottom_im):
    empty = (bottom_re == 0.0) & (bottom_im == 0.0)
    ratio_re, ratio_im = complex_div(
        top_re, top_im, jnp.where(empty, 1.0, bottom_re), bottom_im
    )
    return jnp.where(empty, 0.0, ratio_re), jnp.where(empty, 0.0, ratio_im)


def mode_sines(rows, modes, length):
    product = ((rows + 1)[:, None] * modes[None, :]) % (2 * (length + 1))
    return jnp.sin(product.astype(jnp.float32) * (math.pi / (length + 1))) * math.sqrt(
        2.0 / (length + 1)
    )


def cayley_spectrum(modes, length, diffraction):
    eigenvalue = 4.0 * jnp.sin(modes.astype(jnp.float32) * (math.pi / (2 * (length + 1)))) ** 2
    scaled = diffraction[:, None] * eigenvalue[None, :]
    magnitude = 1.0 + scaled * scaled
    return (1.0 - scaled * scaled) / magnitude, -2.0 * scaled / magnitude


def phased(spectrum, phase_re, phase_im):
    mixed_re, mixed_im = complex_multiply(
        spectrum[..., 0, :, :], spectrum[..., 1, :, :], phase_re, phase_im
    )
    return jnp.stack([mixed_re, mixed_im], axis=-3)


def cayley_rows(values, diffraction):
    length = values.shape[-1]
    counter = lax.optimization_barrier(jnp.arange(length, dtype=jnp.int32))
    if length % 2:
        table = mode_sines(counter, counter + 1, length)
        phase = cayley_spectrum(counter + 1, length, diffraction)
        spectrum = jnp.dot(values, table, precision=HIGH)
        return jnp.dot(phased(spectrum, *phase), table, precision=HIGH)
    half = length // 2
    rows = counter[:half]
    odd_table = mode_sines(rows, 2 * rows + 1, length)
    even_table = mode_sines(rows, 2 * rows + 2, length)
    low = values[..., :half]
    high = jnp.flip(values[..., half:], -1)
    odd = jnp.dot(low + high, odd_table, precision=HIGH)
    even = jnp.dot(low - high, even_table, precision=HIGH)
    odd = phased(odd, *cayley_spectrum(2 * rows + 1, length, diffraction))
    even = phased(even, *cayley_spectrum(2 * rows + 2, length, diffraction))
    back_odd = jnp.einsum("...q,jq->...j", odd, odd_table, precision=HIGH)
    back_even = jnp.einsum("...q,jq->...j", even, even_table, precision=HIGH)
    return jnp.concatenate(
        [back_odd + back_even, jnp.flip(back_odd - back_even, -1)], axis=-1
    )


def shards(beam_field, region_labels, gain_table, diffraction, spectral_weight):
    block, spectra_dev, _, columns = beam_field.shape
    spectra = spectra_dev * lax.axis_size("wl")
    count = lax.axis_size("gx")
    me = lax.axis_index("gx")
    cells = block * count
    regions = gain_table.shape[0]
    region_index = jnp.arange(regions, dtype=jnp.int32)
    base_gain = jnp.sum(
        jnp.where(
            region_labels[None] == region_index[:, None, None], gain_table[:, None, None], 0.0
        ),
        axis=0,
    )

    def power_sum(values):
        return jnp.sum(spectral_weight[None, :, None, None] * (values * values), axis=(1, 2))

    fluence_in = butterfly_sum(power_sum(beam_field), "wl")
    gain_in = base_gain / (1.0 + fluence_in / spectra)
    amplified = with_layout_constraint(
        jnp.transpose(beam_field, (0, 2, 1, 3)) * jnp.exp(0.5 * gain_in)[:, None, None, :],
        Layout(major_to_minor=(0, 1, 2, 3)),
    )

    factor_re, factor_im = inverse_factor(cells, diffraction)
    start = me * block
    around = start - 1 + jnp.arange(block + 2, dtype=jnp.int32)
    around_table = sine_rows(around, cells)
    green_re = jnp.einsum(
        "an,wn,bn->wab", around_table, factor_re, around_table, precision=HIGHEST
    )
    green_im = jnp.einsum(
        "an,wn,bn->wab", around_table, factor_im, around_table, precision=HIGHEST
    )

    def apply_block(rows_re, rows_im, values):
        kernel = jnp.stack(
            [
                jnp.stack([rows_re, -rows_im], axis=2),
                jnp.stack([rows_im, rows_re], axis=2),
            ],
            axis=1,
        )
        return jnp.einsum("wdack,kcwy->adwy", kernel, values, precision=HIGH)

    block_index = jnp.arange(count, dtype=jnp.int32)
    starts = block_index * block
    ends = starts + block - 1
    rise_re, rise_im = safe_ratio(
        *green_entries(ends, ends - block - 1, factor_re, factor_im, cells),
        *green_entries(ends - block, ends - block - 1, factor_re, factor_im, cells),
    )
    fall_re, fall_im = safe_ratio(
        *green_entries(starts, starts + block + 1, factor_re, factor_im, cells),
        *green_entries(starts + block, starts + block + 1, factor_re, factor_im, cells),
    )

    def span_product(ratio_re, ratio_im, first, length):
        total_re = jnp.ones_like(ratio_re[:, 0])
        total_im = jnp.zeros_like(ratio_im[:, 0])
        for offset in range(length):
            pick = jnp.clip(first + offset, 0, count - 1)
            total_re, total_im = complex_multiply(
                total_re, total_im, ratio_re[:, pick], ratio_im[:, pick]
            )
        return total_re[None, :, None], total_im[None, :, None]

    def scale(gain, values):
        moved = complex_multiply(gain[0], gain[1], values[0:1], values[1:2])
        return jnp.concatenate(moved, axis=0)

    along_y = cayley_rows(amplified, diffraction)

    edge_rows = jnp.array([1, block], dtype=jnp.int32)
    edges = apply_block(
        green_re[:, edge_rows, 1 : block + 1], green_im[:, edge_rows, 1 : block + 1], along_y
    )
    from_left = edges[1]
    from_right = edges[0]
    span = 1
    while span < count:
        far_left = shifted(from_left, "gx", span)
        far_right = shifted(from_right, "gx", -span)
        from_left = from_left + scale(span_product(rise_re, rise_im, me - span + 1, span), far_left)
        from_right = from_right + scale(span_product(fall_re, fall_im, me, span), far_right)
        span *= 2
    back_left = safe_ratio(green_re[:, 1, 0], green_im[:, 1, 0], green_re[:, block, 0], green_im[:, block, 0])
    back_right = safe_ratio(
        green_re[:, block, block + 1],
        green_im[:, block, block + 1],
        green_re[:, 1, block + 1],
        green_im[:, 1, block + 1],
    )
    from_left = scale((back_left[0][None, :, None], back_left[1][None, :, None]), from_left - edges[1])
    from_right = scale(
        (back_right[0][None, :, None], back_right[1][None, :, None]), from_right - edges[0]
    )

    local = apply_block(
        green_re[:, 1 : block + 1, 1 : block + 1], green_im[:, 1 : block + 1, 1 : block + 1], along_y
    )
    lead_re, lead_im = safe_ratio(
        green_re[:, 1 : block + 1, 0],
        green_im[:, 1 : block + 1, 0],
        green_re[:, 1:2, 0],
        green_im[:, 1:2, 0],
    )
    trail_re, trail_im = safe_ratio(
        green_re[:, 1 : block + 1, block + 1],
        green_im[:, 1 : block + 1, block + 1],
        green_re[:, block : block + 1, block + 1],
        green_im[:, block : block + 1, block + 1],
    )
    lead = complex_multiply(
        lead_re.T[:, :, None], lead_im.T[:, :, None], from_left[None, 0], from_left[None, 1]
    )
    trail = complex_multiply(
        trail_re.T[:, :, None], trail_im.T[:, :, None], from_right[None, 0], from_right[None, 1]
    )
    solved = local + jnp.stack([lead[0] + trail[0], lead[1] + trail[1]], axis=1)
    result = jnp.transpose(2.0 * solved - along_y, (0, 2, 1, 3))

    fluence_out = butterfly_sum(power_sum(result), "wl")
    gain_out = base_gain / (1.0 + fluence_out / spectra)
    return (result * jnp.exp(0.5 * gain_out)[:, None, None, :], gain_out)


def solution(mesh):
    placed = (P("gx", "wl", None, None), P("gx", None), P(), P("wl"), P("wl"))
    return jax.shard_map(
        shards,
        mesh=mesh,
        in_specs=placed,
        out_specs=(P("gx", "wl", None, None), P("gx", None)),
        check_vma=False,
    )
```

```python
import math

import jax
import jax.numpy as jnp
from jax import lax
from jax.experimental.layout import Layout, with_layout_constraint
from jax.sharding import PartitionSpec as P

HIGHEST = lax.Precision.HIGHEST
HIGH = lax.Precision.HIGH


def complex_multiply(left_re, left_im, right_re, right_im):
    return (left_re * right_re - left_im * right_im, left_re * right_im + left_im * right_re)


def complex_div(top_re, top_im, bottom_re, bottom_im):
    magnitude = bottom_re * bottom_re + bottom_im * bottom_im
    return (
        (top_re * bottom_re + top_im * bottom_im) / magnitude,
        (top_im * bottom_re - top_re * bottom_im) / magnitude,
    )


def sine_rows(index, length):
    mode = jnp.arange(1, length + 1, dtype=jnp.int32)
    product = ((index + 1)[:, None] * mode[None, :]) % (2 * (length + 1))
    value = jnp.sin(product.astype(jnp.float32) * (math.pi / (length + 1))) * math.sqrt(
        2.0 / (length + 1)
    )
    inside = ((index >= 0) & (index < length))[:, None]
    return jnp.where(inside, value, 0.0)


def eigen_scaled(length, diffraction):
    counter = jnp.arange(1, length + 1, dtype=jnp.float32)
    eigenvalue = 4.0 * jnp.sin(counter * (math.pi / (2 * (length + 1)))) ** 2
    return diffraction[:, None] * eigenvalue[None, :]


def inverse_factor(length, diffraction):
    scaled = eigen_scaled(length, diffraction)
    magnitude = 1.0 + scaled * scaled
    return 1.0 / magnitude, -scaled / magnitude


def butterfly_sum(value, axis):
    count = lax.axis_size(axis)
    if count & (count - 1):
        return lax.psum(value, axis)
    step = 1
    while step < count:
        pairs = [(i, i ^ step) for i in range(count)]
        value = value + lax.ppermute(value, axis, pairs)
        step *= 2
    return value


def shifted(value, axis, offset):
    count = lax.axis_size(axis)
    pairs = [(i, i + offset) for i in range(count) if 0 <= i + offset < count]
    return jax.tree.map(lambda part: lax.ppermute(part, axis, pairs), value)


def green_entries(rows, cols, factor_re, factor_im, length):
    row_table = sine_rows(rows, length)
    col_table = sine_rows(cols, length)
    both = row_table * col_table
    return (
        jnp.einsum("mn,wn->wm", both, factor_re, precision=HIGHEST),
        jnp.einsum("mn,wn->wm", both, factor_im, precision=HIGHEST),
    )


def safe_ratio(top_re, top_im, bottom_re, bottom_im):
    empty = (bottom_re == 0.0) & (bottom_im == 0.0)
    ratio_re, ratio_im = complex_div(
        top_re, top_im, jnp.where(empty, 1.0, bottom_re), bottom_im
    )
    return jnp.where(empty, 0.0, ratio_re), jnp.where(empty, 0.0, ratio_im)


def mode_sines(rows, modes, length):
    product = ((rows + 1)[:, None] * modes[None, :]) % (2 * (length + 1))
    return jnp.sin(product.astype(jnp.float32) * (math.pi / (length + 1))) * math.sqrt(
        2.0 / (length + 1)
    )


def cayley_spectrum(modes, length, diffraction):
    eigenvalue = 4.0 * jnp.sin(modes.astype(jnp.float32) * (math.pi / (2 * (length + 1)))) ** 2
    scaled = diffraction[:, None] * eigenvalue[None, :]
    magnitude = 1.0 + scaled * scaled
    return (1.0 - scaled * scaled) / magnitude, -2.0 * scaled / magnitude


def phased(spectrum, phase_re, phase_im):
    mixed_re, mixed_im = complex_multiply(
        spectrum[..., 0, :, :], spectrum[..., 1, :, :], phase_re, phase_im
    )
    return jnp.stack([mixed_re, mixed_im], axis=-3)


def cayley_rows(values, diffraction):
    length = values.shape[-1]
    counter = lax.optimization_barrier(jnp.arange(length, dtype=jnp.int32))
    if length % 2:
        table = mode_sines(counter, counter + 1, length)
        phase = cayley_spectrum(counter + 1, length, diffraction)
        spectrum = jnp.dot(values, table, precision=HIGH)
        return jnp.dot(phased(spectrum, *phase), table, precision=HIGH)
    half = length // 2
    rows = counter[:half]
    odd_table = mode_sines(rows, 2 * rows + 1, length)
    even_table = mode_sines(rows, 2 * rows + 2, length)
    low = values[..., :half]
    high = jnp.flip(values[..., half:], -1)
    odd = jnp.dot(low + high, odd_table, precision=HIGH)
    even = jnp.dot(low - high, even_table, precision=HIGH)
    odd = phased(odd, *cayley_spectrum(2 * rows + 1, length, diffraction))
    even = phased(even, *cayley_spectrum(2 * rows + 2, length, diffraction))
    back_odd = jnp.einsum("...q,jq->...j", odd, odd_table, precision=HIGH)
    back_even = jnp.einsum("...q,jq->...j", even, even_table, precision=HIGH)
    return jnp.concatenate(
        [back_odd + back_even, jnp.flip(back_odd - back_even, -1)], axis=-1
    )


def shards(beam_field, region_labels, gain_table, diffraction, spectral_weight):
    block, spectra_dev, _, columns = beam_field.shape
    spectra = spectra_dev * lax.axis_size("wl")
    count = lax.axis_size("gx")
    me = lax.axis_index("gx")
    cells = block * count
    regions = gain_table.shape[0]
    region_index = jnp.arange(regions, dtype=jnp.int32)
    base_gain = jnp.sum(
        jnp.where(
            region_labels[None] == region_index[:, None, None], gain_table[:, None, None], 0.0
        ),
        axis=0,
    )

    def power_sum(values):
        return jnp.sum(spectral_weight[None, :, None, None] * (values * values), axis=(1, 2))

    fluence_in = butterfly_sum(power_sum(beam_field), "wl")
    gain_in = base_gain / (1.0 + fluence_in / spectra)
    amplified = with_layout_constraint(
        jnp.transpose(beam_field, (0, 2, 1, 3)) * jnp.exp(0.5 * gain_in)[:, None, None, :],
        Layout(major_to_minor=(0, 1, 2, 3)),
    )

    factor_re, factor_im = inverse_factor(cells, diffraction)
    start = me * block
    around = start - 1 + jnp.arange(block + 2, dtype=jnp.int32)
    around_table = sine_rows(around, cells)
    green_re = jnp.einsum(
        "an,wn,bn->wab", around_table, factor_re, around_table, precision=HIGHEST
    )
    green_im = jnp.einsum(
        "an,wn,bn->wab", around_table, factor_im, around_table, precision=HIGHEST
    )

    def apply_block(rows_re, rows_im, values):
        kernel = jnp.stack(
            [
                jnp.stack([rows_re, -rows_im], axis=2),
                jnp.stack([rows_im, rows_re], axis=2),
            ],
            axis=1,
        )
        return jnp.einsum("wdack,kcwy->adwy", kernel, values, precision=HIGH)

    block_index = jnp.arange(count, dtype=jnp.int32)
    starts = block_index * block
    ends = starts + block - 1
    rise_re, rise_im = safe_ratio(
        *green_entries(starts + block, starts - 1, factor_re, factor_im, cells),
        *green_entries(starts, starts - 1, factor_re, factor_im, cells),
    )
    fall_re, fall_im = safe_ratio(
        *green_entries(ends - block, ends + 1, factor_re, factor_im, cells),
        *green_entries(ends, ends + 1, factor_re, factor_im, cells),
    )

    def span_product(ratio_re, ratio_im, first, length):
        total_re = jnp.ones_like(ratio_re[:, 0])
        total_im = jnp.zeros_like(ratio_im[:, 0])
        for offset in range(length):
            pick = jnp.clip(first + offset, 0, count - 1)
            total_re, total_im = complex_multiply(
                total_re, total_im, ratio_re[:, pick], ratio_im[:, pick]
            )
        return total_re[None, :, None], total_im[None, :, None]

    def scale(gain, values):
        moved = complex_multiply(gain[0], gain[1], values[0:1], values[1:2])
        return jnp.concatenate(moved, axis=0)

    along_y = cayley_rows(amplified, diffraction)

    edge_rows = jnp.array([0, block + 1], dtype=jnp.int32)
    edges = apply_block(
        green_re[:, edge_rows, 1 : block + 1], green_im[:, edge_rows, 1 : block + 1], along_y
    )
    from_left = shifted(edges[1], "gx", 1)
    from_right = shifted(edges[0], "gx", -1)
    span = 1
    while span < count - 1:
        far_left = shifted(from_left, "gx", span)
        far_right = shifted(from_right, "gx", -span)
        from_left = from_left + scale(span_product(rise_re, rise_im, me - span, span), far_left)
        from_right = from_right + scale(span_product(fall_re, fall_im, me + 1, span), far_right)
        span *= 2

    local = apply_block(
        green_re[:, 1 : block + 1, 1 : block + 1], green_im[:, 1 : block + 1, 1 : block + 1], along_y
    )
    lead_re, lead_im = safe_ratio(
        green_re[:, 1 : block + 1, 0],
        green_im[:, 1 : block + 1, 0],
        green_re[:, 1:2, 0],
        green_im[:, 1:2, 0],
    )
    trail_re, trail_im = safe_ratio(
        green_re[:, 1 : block + 1, block + 1],
        green_im[:, 1 : block + 1, block + 1],
        green_re[:, block : block + 1, block + 1],
        green_im[:, block : block + 1, block + 1],
    )
    lead = complex_multiply(
        lead_re.T[:, :, None], lead_im.T[:, :, None], from_left[None, 0], from_left[None, 1]
    )
    trail = complex_multiply(
        trail_re.T[:, :, None], trail_im.T[:, :, None], from_right[None, 0], from_right[None, 1]
    )
    solved = local + jnp.stack([lead[0] + trail[0], lead[1] + trail[1]], axis=1)
    result = 2.0 * solved - along_y
    fluence_out = butterfly_sum(
        jnp.sum(spectral_weight[None, None, :, None] * (result * result), axis=(1, 2)), "wl"
    )
    placed = with_layout_constraint(
        jnp.transpose(result, (0, 2, 1, 3)), Layout(major_to_minor=(0, 1, 2, 3))
    )
    gain_out = base_gain / (1.0 + fluence_out / spectra)
    return (placed * jnp.exp(0.5 * gain_out)[:, None, None, :], gain_out)


def solution(mesh):
    placed = (P("gx", "wl", None, None), P("gx", None), P(), P("wl"), P("wl"))
    return jax.shard_map(
        shards,
        mesh=mesh,
        in_specs=placed,
        out_specs=(P("gx", "wl", None, None), P("gx", None)),
        check_vma=False,
    )
```

```python
import math

import jax
import jax.numpy as jnp
from jax import lax
from jax.experimental.layout import Layout, with_layout_constraint
from jax.sharding import PartitionSpec as P

HIGHEST = lax.Precision.HIGHEST
HIGH = lax.Precision.HIGH


def complex_multiply(left_re, left_im, right_re, right_im):
    return (left_re * right_re - left_im * right_im, left_re * right_im + left_im * right_re)


def complex_div(top_re, top_im, bottom_re, bottom_im):
    magnitude = bottom_re * bottom_re + bottom_im * bottom_im
    return (
        (top_re * bottom_re + top_im * bottom_im) / magnitude,
        (top_im * bottom_re - top_re * bottom_im) / magnitude,
    )


def sine_rows(index, length):
    mode = jnp.arange(1, length + 1, dtype=jnp.int32)
    product = ((index + 1)[:, None] * mode[None, :]) % (2 * (length + 1))
    value = jnp.sin(product.astype(jnp.float32) * (math.pi / (length + 1))) * math.sqrt(
        2.0 / (length + 1)
    )
    inside = ((index >= 0) & (index < length))[:, None]
    return jnp.where(inside, value, 0.0)


def eigen_scaled(length, diffraction):
    counter = jnp.arange(1, length + 1, dtype=jnp.float32)
    eigenvalue = 4.0 * jnp.sin(counter * (math.pi / (2 * (length + 1)))) ** 2
    return diffraction[:, None] * eigenvalue[None, :]


def inverse_factor(length, diffraction):
    scaled = eigen_scaled(length, diffraction)
    magnitude = 1.0 + scaled * scaled
    return 1.0 / magnitude, -scaled / magnitude


def butterfly_sum(value, axis, rider):
    count = lax.axis_size(axis)
    if count & (count - 1):
        return lax.optimization_barrier((lax.psum(value, axis), rider))
    step = 1
    while step < count:
        pairs = [(i, i ^ step) for i in range(count)]
        value = value + lax.ppermute(value, axis, pairs)
        if step == 1:
            value, rider = lax.optimization_barrier((value, rider))
        step *= 2
    return value, rider


def shifted(value, axis, offset):
    count = lax.axis_size(axis)
    pairs = [(i, i + offset) for i in range(count) if 0 <= i + offset < count]
    return jax.tree.map(lambda part: lax.ppermute(part, axis, pairs), value)


def green_entries(rows, cols, factor_re, factor_im, length):
    row_table = sine_rows(rows, length)
    col_table = sine_rows(cols, length)
    both = row_table * col_table
    return (
        jnp.einsum("mn,wn->wm", both, factor_re, precision=HIGHEST),
        jnp.einsum("mn,wn->wm", both, factor_im, precision=HIGHEST),
    )


def safe_ratio(top_re, top_im, bottom_re, bottom_im):
    empty = (bottom_re == 0.0) & (bottom_im == 0.0)
    ratio_re, ratio_im = complex_div(
        top_re, top_im, jnp.where(empty, 1.0, bottom_re), bottom_im
    )
    return jnp.where(empty, 0.0, ratio_re), jnp.where(empty, 0.0, ratio_im)


def mode_sines(rows, modes, length):
    product = ((rows + 1)[:, None] * modes[None, :]) % (2 * (length + 1))
    return jnp.sin(product.astype(jnp.float32) * (math.pi / (length + 1))) * math.sqrt(
        2.0 / (length + 1)
    )


def cayley_spectrum(modes, length, diffraction):
    eigenvalue = 4.0 * jnp.sin(modes.astype(jnp.float32) * (math.pi / (2 * (length + 1)))) ** 2
    scaled = diffraction[:, None] * eigenvalue[None, :]
    magnitude = 1.0 + scaled * scaled
    return (1.0 - scaled * scaled) / magnitude, -2.0 * scaled / magnitude


def phased(spectrum, phase_re, phase_im):
    mixed_re, mixed_im = complex_multiply(
        spectrum[..., 0, :, :], spectrum[..., 1, :, :], phase_re, phase_im
    )
    return jnp.stack([mixed_re, mixed_im], axis=-3)


def cayley_rows(values, diffraction, counter):
    length = values.shape[-1]
    if length % 2:
        table = mode_sines(counter, counter + 1, length)
        phase = cayley_spectrum(counter + 1, length, diffraction)
        spectrum = jnp.dot(values, table, precision=HIGH)
        return jnp.dot(phased(spectrum, *phase), table, precision=HIGH)
    half = length // 2
    rows = counter[:half]
    odd_table = mode_sines(rows, 2 * rows + 1, length)
    even_table = mode_sines(rows, 2 * rows + 2, length)
    low = values[..., :half]
    high = jnp.flip(values[..., half:], -1)
    odd = jnp.dot(low + high, odd_table, precision=HIGH)
    even = jnp.dot(low - high, even_table, precision=HIGH)
    odd = phased(odd, *cayley_spectrum(2 * rows + 1, length, diffraction))
    even = phased(even, *cayley_spectrum(2 * rows + 2, length, diffraction))
    back_odd = jnp.einsum("...q,jq->...j", odd, odd_table, precision=HIGH)
    back_even = jnp.einsum("...q,jq->...j", even, even_table, precision=HIGH)
    return jnp.concatenate(
        [back_odd + back_even, jnp.flip(back_odd - back_even, -1)], axis=-1
    )


def shards(beam_field, region_labels, gain_table, diffraction, spectral_weight):
    block, spectra_dev, _, columns = beam_field.shape
    spectra = spectra_dev * lax.axis_size("wl")
    count = lax.axis_size("gx")
    me = lax.axis_index("gx")
    cells = block * count
    regions = gain_table.shape[0]
    region_index = jnp.arange(regions, dtype=jnp.int32)
    base_gain = jnp.sum(
        jnp.where(
            region_labels[None] == region_index[:, None, None], gain_table[:, None, None], 0.0
        ),
        axis=0,
    )

    def power_sum(values):
        return jnp.sum(spectral_weight[None, :, None, None] * (values * values), axis=(1, 2))

    fluence_in, counter = butterfly_sum(
        power_sum(beam_field), "wl", jnp.arange(columns, dtype=jnp.int32)
    )
    gain_in = base_gain / (1.0 + fluence_in / spectra)
    amplified = with_layout_constraint(
        jnp.transpose(beam_field, (0, 2, 1, 3)) * jnp.exp(0.5 * gain_in)[:, None, None, :],
        Layout(major_to_minor=(0, 1, 2, 3)),
    )

    factor_re, factor_im = inverse_factor(cells, diffraction)
    start = me * block
    around = start - 1 + jnp.arange(block + 2, dtype=jnp.int32)
    around_table = sine_rows(around, cells)
    green_re = jnp.einsum(
        "an,wn,bn->wab", around_table, factor_re, around_table, precision=HIGHEST
    )
    green_im = jnp.einsum(
        "an,wn,bn->wab", around_table, factor_im, around_table, precision=HIGHEST
    )

    def apply_block(rows_re, rows_im, values):
        kernel = jnp.stack(
            [
                jnp.stack([rows_re, -rows_im], axis=2),
                jnp.stack([rows_im, rows_re], axis=2),
            ],
            axis=1,
        )
        return jnp.einsum("wdack,kcwy->adwy", kernel, values, precision=HIGH)

    block_index = jnp.arange(count, dtype=jnp.int32)
    starts = block_index * block
    ends = starts + block - 1
    rise_re, rise_im = safe_ratio(
        *green_entries(starts + block, starts - 1, factor_re, factor_im, cells),
        *green_entries(starts, starts - 1, factor_re, factor_im, cells),
    )
    fall_re, fall_im = safe_ratio(
        *green_entries(ends - block, ends + 1, factor_re, factor_im, cells),
        *green_entries(ends, ends + 1, factor_re, factor_im, cells),
    )

    def span_product(ratio_re, ratio_im, first, length):
        total_re = jnp.ones_like(ratio_re[:, 0])
        total_im = jnp.zeros_like(ratio_im[:, 0])
        for offset in range(length):
            pick = jnp.clip(first + offset, 0, count - 1)
            total_re, total_im = complex_multiply(
                total_re, total_im, ratio_re[:, pick], ratio_im[:, pick]
            )
        return total_re[None, :, None], total_im[None, :, None]

    def scale(gain, values):
        moved = complex_multiply(gain[0], gain[1], values[0:1], values[1:2])
        return jnp.concatenate(moved, axis=0)

    along_y = cayley_rows(amplified, diffraction, counter)

    edge_rows = jnp.array([0, block + 1], dtype=jnp.int32)
    edges = apply_block(
        green_re[:, edge_rows, 1 : block + 1], green_im[:, edge_rows, 1 : block + 1], along_y
    )
    from_left = shifted(edges[1], "gx", 1)
    from_right = shifted(edges[0], "gx", -1)
    span = 1
    while span < count - 1:
        far_left = shifted(from_left, "gx", span)
        far_right = shifted(from_right, "gx", -span)
        from_left = from_left + scale(span_product(rise_re, rise_im, me - span, span), far_left)
        from_right = from_right + scale(span_product(fall_re, fall_im, me + 1, span), far_right)
        span *= 2

    local = apply_block(
        green_re[:, 1 : block + 1, 1 : block + 1], green_im[:, 1 : block + 1, 1 : block + 1], along_y
    )
    lead_re, lead_im = safe_ratio(
        green_re[:, 1 : block + 1, 0],
        green_im[:, 1 : block + 1, 0],
        green_re[:, 1:2, 0],
        green_im[:, 1:2, 0],
    )
    trail_re, trail_im = safe_ratio(
        green_re[:, 1 : block + 1, block + 1],
        green_im[:, 1 : block + 1, block + 1],
        green_re[:, block : block + 1, block + 1],
        green_im[:, block : block + 1, block + 1],
    )
    lead = complex_multiply(
        lead_re.T[:, :, None], lead_im.T[:, :, None], from_left[None, 0], from_left[None, 1]
    )
    trail = complex_multiply(
        trail_re.T[:, :, None], trail_im.T[:, :, None], from_right[None, 0], from_right[None, 1]
    )
    solved = local + jnp.stack([lead[0] + trail[0], lead[1] + trail[1]], axis=1)
    result = jnp.transpose(2.0 * solved - along_y, (0, 2, 1, 3))

    fluence_out, _ = butterfly_sum(power_sum(result), "wl", ())
    gain_out = base_gain / (1.0 + fluence_out / spectra)
    return (result * jnp.exp(0.5 * gain_out)[:, None, None, :], gain_out)


def solution(mesh):
    placed = (P("gx", "wl", None, None), P("gx", None), P(), P("wl"), P("wl"))
    return jax.shard_map(
        shards,
        mesh=mesh,
        in_specs=placed,
        out_specs=(P("gx", "wl", None, None), P("gx", None)),
        check_vma=False,
    )
```

```python
import math

import jax
import jax.numpy as jnp
from jax import lax
from jax.experimental.layout import Layout, with_layout_constraint
from jax.sharding import PartitionSpec as P

HIGHEST = lax.Precision.HIGHEST
HIGH = lax.Precision.HIGH


def complex_multiply(left_re, left_im, right_re, right_im):
    return (left_re * right_re - left_im * right_im, left_re * right_im + left_im * right_re)


def complex_div(top_re, top_im, bottom_re, bottom_im):
    magnitude = bottom_re * bottom_re + bottom_im * bottom_im
    return (
        (top_re * bottom_re + top_im * bottom_im) / magnitude,
        (top_im * bottom_re - top_re * bottom_im) / magnitude,
    )


def sine_rows(index, length):
    mode = jnp.arange(1, length + 1, dtype=jnp.int32)
    product = ((index + 1)[:, None] * mode[None, :]) % (2 * (length + 1))
    value = jnp.sin(product.astype(jnp.float32) * (math.pi / (length + 1))) * math.sqrt(
        2.0 / (length + 1)
    )
    inside = ((index >= 0) & (index < length))[:, None]
    return jnp.where(inside, value, 0.0)


def eigen_scaled(length, diffraction):
    counter = jnp.arange(1, length + 1, dtype=jnp.float32)
    eigenvalue = 4.0 * jnp.sin(counter * (math.pi / (2 * (length + 1)))) ** 2
    return diffraction[:, None] * eigenvalue[None, :]


def inverse_factor(length, diffraction):
    scaled = eigen_scaled(length, diffraction)
    magnitude = 1.0 + scaled * scaled
    return 1.0 / magnitude, -scaled / magnitude


def butterfly_sum(value, axis, rider):
    count = lax.axis_size(axis)
    if count & (count - 1):
        return lax.optimization_barrier((lax.psum(value, axis), rider))
    step = 1
    while step < count:
        pairs = [(i, i ^ step) for i in range(count)]
        value = value + lax.ppermute(value, axis, pairs)
        if step == 1:
            value, rider = lax.optimization_barrier((value, rider))
        step *= 2
    return value, rider


def shifted(value, axis, offset):
    count = lax.axis_size(axis)
    pairs = [(i, i + offset) for i in range(count) if 0 <= i + offset < count]
    return jax.tree.map(lambda part: lax.ppermute(part, axis, pairs), value)


def green_entries(rows, cols, factor_re, factor_im, length):
    row_table = sine_rows(rows, length)
    col_table = sine_rows(cols, length)
    both = row_table * col_table
    return (
        jnp.einsum("mn,wn->wm", both, factor_re, precision=HIGHEST),
        jnp.einsum("mn,wn->wm", both, factor_im, precision=HIGHEST),
    )


def safe_ratio(top_re, top_im, bottom_re, bottom_im):
    empty = (bottom_re == 0.0) & (bottom_im == 0.0)
    ratio_re, ratio_im = complex_div(
        top_re, top_im, jnp.where(empty, 1.0, bottom_re), bottom_im
    )
    return jnp.where(empty, 0.0, ratio_re), jnp.where(empty, 0.0, ratio_im)


def mode_sines(rows, modes, length):
    product = ((rows + 1)[:, None] * modes[None, :]) % (2 * (length + 1))
    return jnp.sin(product.astype(jnp.float32) * (math.pi / (length + 1))) * math.sqrt(
        2.0 / (length + 1)
    )


def cayley_spectrum(modes, length, diffraction):
    eigenvalue = 4.0 * jnp.sin(modes.astype(jnp.float32) * (math.pi / (2 * (length + 1)))) ** 2
    scaled = diffraction[:, None] * eigenvalue[None, :]
    magnitude = 1.0 + scaled * scaled
    return (1.0 - scaled * scaled) / magnitude, -2.0 * scaled / magnitude


def phased(spectrum, phase_re, phase_im):
    mixed_re, mixed_im = complex_multiply(
        spectrum[..., 0, :, :], spectrum[..., 1, :, :], phase_re, phase_im
    )
    return jnp.stack([mixed_re, mixed_im], axis=-3)


def cayley_rows(values, diffraction, counter):
    length = values.shape[-1]
    if length % 2:
        table = mode_sines(counter, counter + 1, length)
        phase = cayley_spectrum(counter + 1, length, diffraction)
        spectrum = jnp.dot(values, table, precision=HIGH)
        return jnp.dot(phased(spectrum, *phase), table, precision=HIGH), None
    half = length // 2
    rows = counter[:half]
    odd_table = mode_sines(rows, 2 * rows + 1, length)
    even_table = mode_sines(rows, 2 * rows + 2, length)
    low = values[..., :half]
    high = jnp.flip(values[..., half:], -1)
    odd = jnp.dot(low + high, odd_table, precision=HIGH)
    even = jnp.dot(low - high, even_table, precision=HIGH)
    odd = phased(odd, *cayley_spectrum(2 * rows + 1, length, diffraction))
    even = phased(even, *cayley_spectrum(2 * rows + 2, length, diffraction))
    back_odd = jnp.einsum("...q,jq->...j", odd, odd_table, precision=HIGH)
    back_even = jnp.einsum("...q,jq->...j", even, even_table, precision=HIGH)
    return back_odd + back_even, back_odd - back_even


def shards(beam_field, region_labels, gain_table, diffraction, spectral_weight):
    block, spectra_dev, _, columns = beam_field.shape
    spectra = spectra_dev * lax.axis_size("wl")
    count = lax.axis_size("gx")
    me = lax.axis_index("gx")
    cells = block * count
    regions = gain_table.shape[0]
    region_index = jnp.arange(regions, dtype=jnp.int32)
    base_gain = jnp.sum(
        jnp.where(
            region_labels[None] == region_index[:, None, None], gain_table[:, None, None], 0.0
        ),
        axis=0,
    )

    def power_sum(values):
        return jnp.sum(spectral_weight[None, :, None, None] * (values * values), axis=(1, 2))

    fluence_in, counter = butterfly_sum(
        power_sum(beam_field), "wl", jnp.arange(columns, dtype=jnp.int32)
    )
    gain_in = base_gain / (1.0 + fluence_in / spectra)
    amplified = with_layout_constraint(
        jnp.transpose(beam_field, (0, 2, 1, 3)) * jnp.exp(0.5 * gain_in)[:, None, None, :],
        Layout(major_to_minor=(0, 1, 2, 3)),
    )

    factor_re, factor_im = inverse_factor(cells, diffraction)
    start = me * block
    around = start - 1 + jnp.arange(block + 2, dtype=jnp.int32)
    around_table = sine_rows(around, cells)
    green_re = jnp.einsum(
        "an,wn,bn->wab", around_table, factor_re, around_table, precision=HIGHEST
    )
    green_im = jnp.einsum(
        "an,wn,bn->wab", around_table, factor_im, around_table, precision=HIGHEST
    )

    def apply_block(rows_re, rows_im, values):
        kernel = jnp.stack(
            [
                jnp.stack([rows_re, -rows_im], axis=2),
                jnp.stack([rows_im, rows_re], axis=2),
            ],
            axis=1,
        )
        return jnp.einsum("wdack,kcwy->adwy", kernel, values, precision=HIGH)

    block_index = jnp.arange(count, dtype=jnp.int32)
    starts = block_index * block
    ends = starts + block - 1
    rise_re, rise_im = safe_ratio(
        *green_entries(starts + block, starts - 1, factor_re, factor_im, cells),
        *green_entries(starts, starts - 1, factor_re, factor_im, cells),
    )
    fall_re, fall_im = safe_ratio(
        *green_entries(ends - block, ends + 1, factor_re, factor_im, cells),
        *green_entries(ends, ends + 1, factor_re, factor_im, cells),
    )

    def span_product(ratio_re, ratio_im, first, length):
        total_re = jnp.ones_like(ratio_re[:, 0])
        total_im = jnp.zeros_like(ratio_im[:, 0])
        for offset in range(length):
            pick = jnp.clip(first + offset, 0, count - 1)
            total_re, total_im = complex_multiply(
                total_re, total_im, ratio_re[:, pick], ratio_im[:, pick]
            )
        return total_re[None, :, None], total_im[None, :, None]

    def scale(gain, values):
        moved = complex_multiply(gain[0], gain[1], values[0:1], values[1:2])
        return jnp.concatenate(moved, axis=0)

    first, second = cayley_rows(amplified, diffraction, counter)

    def joined(values, reversed_half):
        if reversed_half is None:
            return values
        return jnp.concatenate([values, jnp.flip(reversed_half, -1)], axis=-1)

    edge_re = jnp.concatenate([green_re[:, 0:1, 1 : block + 1], green_re[:, block + 1 :, 1 : block + 1]], axis=1)
    edge_im = jnp.concatenate([green_im[:, 0:1, 1 : block + 1], green_im[:, block + 1 :, 1 : block + 1]], axis=1)
    edges = joined(
        apply_block(edge_re, edge_im, first),
        None if second is None else apply_block(edge_re, edge_im, second),
    )
    along_y = joined(first, second)
    from_left = shifted(edges[1], "gx", 1)
    from_right = shifted(edges[0], "gx", -1)
    span = 1
    while span < count - 1:
        far_left = shifted(from_left, "gx", span)
        far_right = shifted(from_right, "gx", -span)
        from_left = from_left + scale(span_product(rise_re, rise_im, me - span, span), far_left)
        from_right = from_right + scale(span_product(fall_re, fall_im, me + 1, span), far_right)
        span *= 2

    local = apply_block(
        green_re[:, 1 : block + 1, 1 : block + 1], green_im[:, 1 : block + 1, 1 : block + 1], along_y
    )
    lead_re, lead_im = safe_ratio(
        green_re[:, 1 : block + 1, 0],
        green_im[:, 1 : block + 1, 0],
        green_re[:, 1:2, 0],
        green_im[:, 1:2, 0],
    )
    trail_re, trail_im = safe_ratio(
        green_re[:, 1 : block + 1, block + 1],
        green_im[:, 1 : block + 1, block + 1],
        green_re[:, block : block + 1, block + 1],
        green_im[:, block : block + 1, block + 1],
    )
    lead = complex_multiply(
        lead_re.T[:, :, None], lead_im.T[:, :, None], from_left[None, 0], from_left[None, 1]
    )
    trail = complex_multiply(
        trail_re.T[:, :, None], trail_im.T[:, :, None], from_right[None, 0], from_right[None, 1]
    )
    solved = local + jnp.stack([lead[0] + trail[0], lead[1] + trail[1]], axis=1)
    result = jnp.transpose(2.0 * solved - along_y, (0, 2, 1, 3))

    fluence_out, _ = butterfly_sum(power_sum(result), "wl", ())
    gain_out = base_gain / (1.0 + fluence_out / spectra)
    return (result * jnp.exp(0.5 * gain_out)[:, None, None, :], gain_out)


def solution(mesh):
    placed = (P("gx", "wl", None, None), P("gx", None), P(), P("wl"), P("wl"))
    return jax.shard_map(
        shards,
        mesh=mesh,
        in_specs=placed,
        out_specs=(P("gx", "wl", None, None), P("gx", None)),
        check_vma=False,
    )
```

```python
import math

import jax
import jax.numpy as jnp
from jax import lax
from jax.experimental.layout import Layout, with_layout_constraint
from jax.sharding import PartitionSpec as P

HIGHEST = lax.Precision.HIGHEST
HIGH = lax.Precision.HIGH


def complex_multiply(left_re, left_im, right_re, right_im):
    return (left_re * right_re - left_im * right_im, left_re * right_im + left_im * right_re)


def complex_div(top_re, top_im, bottom_re, bottom_im):
    magnitude = bottom_re * bottom_re + bottom_im * bottom_im
    return (
        (top_re * bottom_re + top_im * bottom_im) / magnitude,
        (top_im * bottom_re - top_re * bottom_im) / magnitude,
    )


def sine_rows(index, length):
    mode = jnp.arange(1, length + 1, dtype=jnp.int32)
    product = ((index + 1)[:, None] * mode[None, :]) % (2 * (length + 1))
    value = jnp.sin(product.astype(jnp.float32) * (math.pi / (length + 1))) * math.sqrt(
        2.0 / (length + 1)
    )
    inside = ((index >= 0) & (index < length))[:, None]
    return jnp.where(inside, value, 0.0)


def eigen_scaled(length, diffraction):
    counter = jnp.arange(1, length + 1, dtype=jnp.float32)
    eigenvalue = 4.0 * jnp.sin(counter * (math.pi / (2 * (length + 1)))) ** 2
    return diffraction[:, None] * eigenvalue[None, :]


def inverse_factor(length, diffraction):
    scaled = eigen_scaled(length, diffraction)
    magnitude = 1.0 + scaled * scaled
    return 1.0 / magnitude, -scaled / magnitude


def butterfly_sum(value, axis, rider):
    count = lax.axis_size(axis)
    if count & (count - 1):
        return lax.optimization_barrier((lax.psum(value, axis), rider))
    step = 1
    while step < count:
        pairs = [(i, i ^ step) for i in range(count)]
        value = value + lax.ppermute(value, axis, pairs)
        if step == 1:
            value, rider = lax.optimization_barrier((value, rider))
        step *= 2
    return value, rider


def shifted(value, axis, offset):
    count = lax.axis_size(axis)
    pairs = [(i, i + offset) for i in range(count) if 0 <= i + offset < count]
    return jax.tree.map(lambda part: lax.ppermute(part, axis, pairs), value)


def green_entries(rows, cols, factor_re, factor_im, length):
    row_table = sine_rows(rows, length)
    col_table = sine_rows(cols, length)
    both = row_table * col_table
    return (
        jnp.einsum("mn,wn->wm", both, factor_re, precision=HIGHEST),
        jnp.einsum("mn,wn->wm", both, factor_im, precision=HIGHEST),
    )


def safe_ratio(top_re, top_im, bottom_re, bottom_im):
    empty = (bottom_re == 0.0) & (bottom_im == 0.0)
    ratio_re, ratio_im = complex_div(
        top_re, top_im, jnp.where(empty, 1.0, bottom_re), bottom_im
    )
    return jnp.where(empty, 0.0, ratio_re), jnp.where(empty, 0.0, ratio_im)


def mode_sines(rows, modes, length):
    product = ((rows + 1)[:, None] * modes[None, :]) % (2 * (length + 1))
    return jnp.sin(product.astype(jnp.float32) * (math.pi / (length + 1))) * math.sqrt(
        2.0 / (length + 1)
    )


def cayley_spectrum(modes, length, diffraction):
    eigenvalue = 4.0 * jnp.sin(modes.astype(jnp.float32) * (math.pi / (2 * (length + 1)))) ** 2
    scaled = diffraction[:, None] * eigenvalue[None, :]
    magnitude = 1.0 + scaled * scaled
    return (1.0 - scaled * scaled) / magnitude, -2.0 * scaled / magnitude


def phased(spectrum, phase_re, phase_im):
    mixed_re, mixed_im = complex_multiply(
        spectrum[..., 0, :, :], spectrum[..., 1, :, :], phase_re, phase_im
    )
    return jnp.stack([mixed_re, mixed_im], axis=-3)


def cayley_rows(values, diffraction, counter):
    length = values.shape[-1]
    if length % 2:
        table = mode_sines(counter, counter + 1, length)
        phase = cayley_spectrum(counter + 1, length, diffraction)
        spectrum = jnp.dot(values, table, precision=HIGH)
        return jnp.dot(phased(spectrum, *phase), table, precision=HIGH), None, None
    half = length // 2
    rows = counter[:half]
    odd_table = mode_sines(rows, 2 * rows + 1, length)
    even_table = mode_sines(rows, 2 * rows + 2, length)
    low = values[..., :half]
    high = jnp.flip(values[..., half:], -1)
    odd = jnp.dot(low + high, odd_table, precision=HIGH)
    even = jnp.dot(low - high, even_table, precision=HIGH)
    odd = phased(odd, *cayley_spectrum(2 * rows + 1, length, diffraction))
    even = phased(even, *cayley_spectrum(2 * rows + 2, length, diffraction))
    back_odd = jnp.einsum("...q,jq->...j", odd, odd_table, precision=HIGH)
    back_even = jnp.einsum("...q,jq->...j", even, even_table, precision=HIGH)
    return back_odd + back_even, back_odd - back_even, (odd, even, odd_table, even_table)


def small_back(values, table):
    flat = values.reshape(-1, values.shape[-1])
    return jnp.dot(table, flat.T, precision=HIGH).T.reshape(values.shape[:-1] + (table.shape[0],))


def shards(beam_field, region_labels, gain_table, diffraction, spectral_weight):
    block, spectra_dev, _, columns = beam_field.shape
    spectra = spectra_dev * lax.axis_size("wl")
    count = lax.axis_size("gx")
    me = lax.axis_index("gx")
    cells = block * count
    regions = gain_table.shape[0]
    region_index = jnp.arange(regions, dtype=jnp.int32)
    base_gain = jnp.sum(
        jnp.where(
            region_labels[None] == region_index[:, None, None], gain_table[:, None, None], 0.0
        ),
        axis=0,
    )

    def power_sum(values):
        return jnp.sum(spectral_weight[None, :, None, None] * (values * values), axis=(1, 2))

    fluence_in, counter = butterfly_sum(
        power_sum(beam_field), "wl", jnp.arange(columns, dtype=jnp.int32)
    )
    gain_in = base_gain / (1.0 + fluence_in / spectra)
    amplified = with_layout_constraint(
        jnp.transpose(beam_field, (0, 2, 1, 3)) * jnp.exp(0.5 * gain_in)[:, None, None, :],
        Layout(major_to_minor=(0, 1, 2, 3)),
    )

    factor_re, factor_im = inverse_factor(cells, diffraction)
    start = me * block
    around = start - 1 + jnp.arange(block + 2, dtype=jnp.int32)
    around_table = sine_rows(around, cells)
    green_re = jnp.einsum(
        "an,wn,bn->wab", around_table, factor_re, around_table, precision=HIGHEST
    )
    green_im = jnp.einsum(
        "an,wn,bn->wab", around_table, factor_im, around_table, precision=HIGHEST
    )

    def apply_block(rows_re, rows_im, values):
        kernel = jnp.stack(
            [
                jnp.stack([rows_re, -rows_im], axis=2),
                jnp.stack([rows_im, rows_re], axis=2),
            ],
            axis=1,
        )
        return jnp.einsum("wdack,kcwy->adwy", kernel, values, precision=HIGH)

    block_index = jnp.arange(count, dtype=jnp.int32)
    starts = block_index * block
    ends = starts + block - 1
    rise_re, rise_im = safe_ratio(
        *green_entries(starts + block, starts - 1, factor_re, factor_im, cells),
        *green_entries(starts, starts - 1, factor_re, factor_im, cells),
    )
    fall_re, fall_im = safe_ratio(
        *green_entries(ends - block, ends + 1, factor_re, factor_im, cells),
        *green_entries(ends, ends + 1, factor_re, factor_im, cells),
    )

    def span_product(ratio_re, ratio_im, first, length):
        total_re = jnp.ones_like(ratio_re[:, 0])
        total_im = jnp.zeros_like(ratio_im[:, 0])
        for offset in range(length):
            pick = jnp.clip(first + offset, 0, count - 1)
            total_re, total_im = complex_multiply(
                total_re, total_im, ratio_re[:, pick], ratio_im[:, pick]
            )
        return total_re[None, :, None], total_im[None, :, None]

    def scale(gain, values):
        moved = complex_multiply(gain[0], gain[1], values[0:1], values[1:2])
        return jnp.concatenate(moved, axis=0)

    first, second, spectral = cayley_rows(amplified, diffraction, counter)

    def joined(values, reversed_half):
        if reversed_half is None:
            return values
        return jnp.concatenate([values, jnp.flip(reversed_half, -1)], axis=-1)

    edge_re = jnp.concatenate([green_re[:, 0:1, 1 : block + 1], green_re[:, block + 1 :, 1 : block + 1]], axis=1)
    edge_im = jnp.concatenate([green_im[:, 0:1, 1 : block + 1], green_im[:, block + 1 :, 1 : block + 1]], axis=1)
    if spectral is None:
        edges = apply_block(edge_re, edge_im, first)
    else:
        odd, even, odd_table, even_table = spectral
        edge_odd = small_back(apply_block(edge_re, edge_im, odd), odd_table)
        edge_even = small_back(apply_block(edge_re, edge_im, even), even_table)
        edges = joined(edge_odd + edge_even, edge_odd - edge_even)
    along_y = joined(first, second)
    from_left = shifted(edges[1], "gx", 1)
    from_right = shifted(edges[0], "gx", -1)
    span = 1
    while span < count - 1:
        far_left = shifted(from_left, "gx", span)
        far_right = shifted(from_right, "gx", -span)
        from_left = from_left + scale(span_product(rise_re, rise_im, me - span, span), far_left)
        from_right = from_right + scale(span_product(fall_re, fall_im, me + 1, span), far_right)
        span *= 2

    local = apply_block(
        green_re[:, 1 : block + 1, 1 : block + 1], green_im[:, 1 : block + 1, 1 : block + 1], along_y
    )
    lead_re, lead_im = safe_ratio(
        green_re[:, 1 : block + 1, 0],
        green_im[:, 1 : block + 1, 0],
        green_re[:, 1:2, 0],
        green_im[:, 1:2, 0],
    )
    trail_re, trail_im = safe_ratio(
        green_re[:, 1 : block + 1, block + 1],
        green_im[:, 1 : block + 1, block + 1],
        green_re[:, block : block + 1, block + 1],
        green_im[:, block : block + 1, block + 1],
    )
    lead = complex_multiply(
        lead_re.T[:, :, None], lead_im.T[:, :, None], from_left[None, 0], from_left[None, 1]
    )
    trail = complex_multiply(
        trail_re.T[:, :, None], trail_im.T[:, :, None], from_right[None, 0], from_right[None, 1]
    )
    solved = local + jnp.stack([lead[0] + trail[0], lead[1] + trail[1]], axis=1)
    result = jnp.transpose(2.0 * solved - along_y, (0, 2, 1, 3))

    fluence_out, _ = butterfly_sum(power_sum(result), "wl", ())
    gain_out = base_gain / (1.0 + fluence_out / spectra)
    return (result * jnp.exp(0.5 * gain_out)[:, None, None, :], gain_out)


def solution(mesh):
    placed = (P("gx", "wl", None, None), P("gx", None), P(), P("wl"), P("wl"))
    return jax.shard_map(
        shards,
        mesh=mesh,
        in_specs=placed,
        out_specs=(P("gx", "wl", None, None), P("gx", None)),
        check_vma=False,
    )
```

```python
import math

import jax
import jax.numpy as jnp
from jax import lax
from jax.experimental.layout import Layout, with_layout_constraint
from jax.sharding import PartitionSpec as P

HIGHEST = lax.Precision.HIGHEST
HIGH = lax.Precision.HIGH


def complex_multiply(left_re, left_im, right_re, right_im):
    return (left_re * right_re - left_im * right_im, left_re * right_im + left_im * right_re)


def complex_div(top_re, top_im, bottom_re, bottom_im):
    magnitude = bottom_re * bottom_re + bottom_im * bottom_im
    return (
        (top_re * bottom_re + top_im * bottom_im) / magnitude,
        (top_im * bottom_re - top_re * bottom_im) / magnitude,
    )


def sine_rows(index, length):
    mode = jnp.arange(1, length + 1, dtype=jnp.int32)
    product = ((index + 1)[:, None] * mode[None, :]) % (2 * (length + 1))
    value = jnp.sin(product.astype(jnp.float32) * (math.pi / (length + 1))) * math.sqrt(
        2.0 / (length + 1)
    )
    inside = ((index >= 0) & (index < length))[:, None]
    return jnp.where(inside, value, 0.0)


def eigen_scaled(length, diffraction):
    counter = jnp.arange(1, length + 1, dtype=jnp.float32)
    eigenvalue = 4.0 * jnp.sin(counter * (math.pi / (2 * (length + 1)))) ** 2
    return diffraction[:, None] * eigenvalue[None, :]


def inverse_factor(length, diffraction):
    scaled = eigen_scaled(length, diffraction)
    magnitude = 1.0 + scaled * scaled
    return 1.0 / magnitude, -scaled / magnitude


def butterfly_sum(value, axis, rider):
    count = lax.axis_size(axis)
    if count & (count - 1):
        return lax.optimization_barrier((lax.psum(value, axis), rider))
    step = 1
    while step < count:
        pairs = [(i, i ^ step) for i in range(count)]
        value = value + lax.ppermute(value, axis, pairs)
        if step == 1:
            value, rider = lax.optimization_barrier((value, rider))
        step *= 2
    return value, rider


def shifted(value, axis, offset):
    count = lax.axis_size(axis)
    pairs = [(i, i + offset) for i in range(count) if 0 <= i + offset < count]
    return jax.tree.map(lambda part: lax.ppermute(part, axis, pairs), value)


def green_entries(rows, cols, factor_re, factor_im, length):
    row_table = sine_rows(rows, length)
    col_table = sine_rows(cols, length)
    both = row_table * col_table
    return (
        jnp.einsum("mn,wn->wm", both, factor_re, precision=HIGHEST),
        jnp.einsum("mn,wn->wm", both, factor_im, precision=HIGHEST),
    )


def safe_ratio(top_re, top_im, bottom_re, bottom_im):
    empty = (bottom_re == 0.0) & (bottom_im == 0.0)
    ratio_re, ratio_im = complex_div(
        top_re, top_im, jnp.where(empty, 1.0, bottom_re), bottom_im
    )
    return jnp.where(empty, 0.0, ratio_re), jnp.where(empty, 0.0, ratio_im)


def mode_sines(rows, modes, length):
    product = ((rows + 1)[:, None] * modes[None, :]) % (2 * (length + 1))
    return jnp.sin(product.astype(jnp.float32) * (math.pi / (length + 1))) * math.sqrt(
        2.0 / (length + 1)
    )


def cayley_spectrum(modes, length, diffraction):
    eigenvalue = 4.0 * jnp.sin(modes.astype(jnp.float32) * (math.pi / (2 * (length + 1)))) ** 2
    scaled = diffraction[:, None] * eigenvalue[None, :]
    magnitude = 1.0 + scaled * scaled
    return (1.0 - scaled * scaled) / magnitude, -2.0 * scaled / magnitude


def phased(spectrum, phase_re, phase_im):
    mixed_re, mixed_im = complex_multiply(
        spectrum[..., 0, :, :], spectrum[..., 1, :, :], phase_re, phase_im
    )
    return jnp.stack([mixed_re, mixed_im], axis=-3)


def cayley_rows(values, diffraction, counter):
    length = values.shape[-1]
    if length % 2:
        table = mode_sines(counter, counter + 1, length)
        phase = cayley_spectrum(counter + 1, length, diffraction)
        spectrum = jnp.dot(values, table, precision=HIGH)
        return jnp.dot(phased(spectrum, *phase), table, precision=HIGH), None
    half = length // 2
    rows = counter[:half]
    odd_table = mode_sines(rows, 2 * rows + 1, length)
    even_table = mode_sines(rows, 2 * rows + 2, length)
    low = values[..., :half]
    high = jnp.flip(values[..., half:], -1)
    odd = jnp.dot(low + high, odd_table, precision=HIGH)
    even = jnp.dot(low - high, even_table, precision=HIGH)
    odd = phased(odd, *cayley_spectrum(2 * rows + 1, length, diffraction))
    even = phased(even, *cayley_spectrum(2 * rows + 2, length, diffraction))
    back_odd = jnp.einsum("...q,jq->...j", odd, odd_table, precision=HIGH)
    back_even = jnp.einsum("...q,jq->...j", even, even_table, precision=HIGH)
    return back_odd + back_even, back_odd - back_even


def shards(beam_field, region_labels, gain_table, diffraction, spectral_weight):
    block, spectra_dev, _, columns = beam_field.shape
    spectra = spectra_dev * lax.axis_size("wl")
    count = lax.axis_size("gx")
    me = lax.axis_index("gx")
    cells = block * count
    regions = gain_table.shape[0]
    region_index = jnp.arange(regions, dtype=jnp.int32)
    base_gain = jnp.sum(
        jnp.where(
            region_labels[None] == region_index[:, None, None], gain_table[:, None, None], 0.0
        ),
        axis=0,
    )

    def power_sum(values):
        return jnp.sum(spectral_weight[None, :, None, None] * (values * values), axis=(1, 2))

    fluence_in, counter = butterfly_sum(
        power_sum(beam_field), "wl", jnp.arange(columns, dtype=jnp.int32)
    )
    gain_in = base_gain / (1.0 + fluence_in / spectra)
    amplified = with_layout_constraint(
        jnp.transpose(beam_field, (0, 2, 1, 3)) * jnp.exp(0.5 * gain_in)[:, None, None, :],
        Layout(major_to_minor=(0, 1, 2, 3)),
    )

    factor_re, factor_im = inverse_factor(cells, diffraction)
    start = me * block
    around = start - 1 + jnp.arange(block + 2, dtype=jnp.int32)
    around_table = sine_rows(around, cells)
    green_re = jnp.einsum(
        "an,wn,bn->wab", around_table, factor_re, around_table, precision=HIGHEST
    )
    green_im = jnp.einsum(
        "an,wn,bn->wab", around_table, factor_im, around_table, precision=HIGHEST
    )

    def apply_block(rows_re, rows_im, values):
        kernel = jnp.stack(
            [
                jnp.stack([rows_re, -rows_im], axis=2),
                jnp.stack([rows_im, rows_re], axis=2),
            ],
            axis=1,
        )
        return jnp.einsum("wdack,kcwy->adwy", kernel, values, precision=HIGH)

    block_index = jnp.arange(count, dtype=jnp.int32)
    starts = block_index * block
    ends = starts + block - 1
    rise_re, rise_im = safe_ratio(
        *green_entries(starts + block, starts - 1, factor_re, factor_im, cells),
        *green_entries(starts, starts - 1, factor_re, factor_im, cells),
    )
    fall_re, fall_im = safe_ratio(
        *green_entries(ends - block, ends + 1, factor_re, factor_im, cells),
        *green_entries(ends, ends + 1, factor_re, factor_im, cells),
    )

    def span_product(ratio_re, ratio_im, first, length):
        total_re = jnp.ones_like(ratio_re[:, 0])
        total_im = jnp.zeros_like(ratio_im[:, 0])
        for offset in range(length):
            pick = jnp.clip(first + offset, 0, count - 1)
            total_re, total_im = complex_multiply(
                total_re, total_im, ratio_re[:, pick], ratio_im[:, pick]
            )
        return total_re[None, :, None], total_im[None, :, None]

    def scale(gain, values):
        moved = complex_multiply(gain[0], gain[1], values[0:1], values[1:2])
        return jnp.concatenate(moved, axis=0)

    first, second = cayley_rows(amplified, diffraction, counter)

    def joined(values, reversed_half):
        if reversed_half is None:
            return values
        return jnp.concatenate([values, jnp.flip(reversed_half, -1)], axis=-1)

    edge_re = jnp.concatenate([green_re[:, 0:1, 1 : block + 1], green_re[:, block + 1 :, 1 : block + 1]], axis=1)
    edge_im = jnp.concatenate([green_im[:, 0:1, 1 : block + 1], green_im[:, block + 1 :, 1 : block + 1]], axis=1)
    edges = joined(
        apply_block(edge_re, edge_im, first),
        None if second is None else apply_block(edge_re, edge_im, second),
    )
    from_left = shifted(edges[1], "gx", 1)
    from_right = shifted(edges[0], "gx", -1)
    span = 1
    while span < count - 1:
        far_left = shifted(from_left, "gx", span)
        far_right = shifted(from_right, "gx", -span)
        from_left = from_left + scale(span_product(rise_re, rise_im, me - span, span), far_left)
        from_right = from_right + scale(span_product(fall_re, fall_im, me + 1, span), far_right)
        if span == 1:
            from_left, from_right, first, second = lax.optimization_barrier(
                (from_left, from_right, first, second)
            )
        span *= 2
    along_y = joined(first, second)

    local = apply_block(
        green_re[:, 1 : block + 1, 1 : block + 1], green_im[:, 1 : block + 1, 1 : block + 1], along_y
    )
    lead_re, lead_im = safe_ratio(
        green_re[:, 1 : block + 1, 0],
        green_im[:, 1 : block + 1, 0],
        green_re[:, 1:2, 0],
        green_im[:, 1:2, 0],
    )
    trail_re, trail_im = safe_ratio(
        green_re[:, 1 : block + 1, block + 1],
        green_im[:, 1 : block + 1, block + 1],
        green_re[:, block : block + 1, block + 1],
        green_im[:, block : block + 1, block + 1],
    )
    lead = complex_multiply(
        lead_re.T[:, :, None], lead_im.T[:, :, None], from_left[None, 0], from_left[None, 1]
    )
    trail = complex_multiply(
        trail_re.T[:, :, None], trail_im.T[:, :, None], from_right[None, 0], from_right[None, 1]
    )
    solved = local + jnp.stack([lead[0] + trail[0], lead[1] + trail[1]], axis=1)
    result = jnp.transpose(2.0 * solved - along_y, (0, 2, 1, 3))

    fluence_out, _ = butterfly_sum(power_sum(result), "wl", ())
    gain_out = base_gain / (1.0 + fluence_out / spectra)
    return (result * jnp.exp(0.5 * gain_out)[:, None, None, :], gain_out)


def solution(mesh):
    placed = (P("gx", "wl", None, None), P("gx", None), P(), P("wl"), P("wl"))
    return jax.shard_map(
        shards,
        mesh=mesh,
        in_specs=placed,
        out_specs=(P("gx", "wl", None, None), P("gx", None)),
        check_vma=False,
    )
```

```python
import math

import jax
import jax.numpy as jnp
from jax import lax
from jax.experimental.layout import Layout, with_layout_constraint
from jax.sharding import PartitionSpec as P

HIGHEST = lax.Precision.HIGHEST
HIGH = lax.Precision.HIGH


def complex_multiply(left_re, left_im, right_re, right_im):
    return (left_re * right_re - left_im * right_im, left_re * right_im + left_im * right_re)


def complex_div(top_re, top_im, bottom_re, bottom_im):
    magnitude = bottom_re * bottom_re + bottom_im * bottom_im
    return (
        (top_re * bottom_re + top_im * bottom_im) / magnitude,
        (top_im * bottom_re - top_re * bottom_im) / magnitude,
    )


def sine_rows(index, length):
    mode = jnp.arange(1, length + 1, dtype=jnp.int32)
    product = ((index + 1)[:, None] * mode[None, :]) % (2 * (length + 1))
    value = jnp.sin(product.astype(jnp.float32) * (math.pi / (length + 1))) * math.sqrt(
        2.0 / (length + 1)
    )
    inside = ((index >= 0) & (index < length))[:, None]
    return jnp.where(inside, value, 0.0)


def eigen_scaled(length, diffraction):
    counter = jnp.arange(1, length + 1, dtype=jnp.float32)
    eigenvalue = 4.0 * jnp.sin(counter * (math.pi / (2 * (length + 1)))) ** 2
    return diffraction[:, None] * eigenvalue[None, :]


def inverse_factor(length, diffraction):
    scaled = eigen_scaled(length, diffraction)
    magnitude = 1.0 + scaled * scaled
    return 1.0 / magnitude, -scaled / magnitude


def butterfly_sum(value, axis, rider):
    count = lax.axis_size(axis)
    if count & (count - 1):
        return lax.optimization_barrier((lax.psum(value, axis), rider))
    step = 1
    while step < count:
        pairs = [(i, i ^ step) for i in range(count)]
        value = value + lax.ppermute(value, axis, pairs)
        if step == 1:
            value, rider = lax.optimization_barrier((value, rider))
        step *= 2
    return value, rider


def shifted(value, axis, offset):
    count = lax.axis_size(axis)
    pairs = [(i, i + offset) for i in range(count) if 0 <= i + offset < count]
    return jax.tree.map(lambda part: lax.ppermute(part, axis, pairs), value)


def green_entries(rows, cols, factor_re, factor_im, length):
    row_table = sine_rows(rows, length)
    col_table = sine_rows(cols, length)
    both = row_table * col_table
    return (
        jnp.einsum("mn,wn->wm", both, factor_re, precision=HIGHEST),
        jnp.einsum("mn,wn->wm", both, factor_im, precision=HIGHEST),
    )


def safe_ratio(top_re, top_im, bottom_re, bottom_im):
    empty = (bottom_re == 0.0) & (bottom_im == 0.0)
    ratio_re, ratio_im = complex_div(
        top_re, top_im, jnp.where(empty, 1.0, bottom_re), bottom_im
    )
    return jnp.where(empty, 0.0, ratio_re), jnp.where(empty, 0.0, ratio_im)


def mode_sines(rows, modes, length):
    product = ((rows + 1)[:, None] * modes[None, :]) % (2 * (length + 1))
    return jnp.sin(product.astype(jnp.float32) * (math.pi / (length + 1))) * math.sqrt(
        2.0 / (length + 1)
    )


def cayley_spectrum(modes, length, diffraction):
    eigenvalue = 4.0 * jnp.sin(modes.astype(jnp.float32) * (math.pi / (2 * (length + 1)))) ** 2
    scaled = diffraction[:, None] * eigenvalue[None, :]
    magnitude = 1.0 + scaled * scaled
    return (1.0 - scaled * scaled) / magnitude, -2.0 * scaled / magnitude


def phased(spectrum, phase_re, phase_im):
    mixed_re, mixed_im = complex_multiply(
        spectrum[..., 0, :, :], spectrum[..., 1, :, :], phase_re, phase_im
    )
    return jnp.stack([mixed_re, mixed_im], axis=-3)


def cayley_rows(values, diffraction, counter):
    length = counter.shape[0]
    if length % 2:
        table = mode_sines(counter, counter + 1, length)
        phase = cayley_spectrum(counter + 1, length, diffraction)
        spectrum = jnp.dot(values, table, precision=HIGH)
        return jnp.dot(phased(spectrum, *phase), table, precision=HIGH), None
    half = length // 2
    rows = counter[:half]
    odd_table = mode_sines(rows, 2 * rows + 1, length)
    even_table = mode_sines(rows, 2 * rows + 2, length)
    total, difference = values
    odd = jnp.dot(total, odd_table, precision=HIGH)
    even = jnp.dot(difference, even_table, precision=HIGH)
    odd = phased(odd, *cayley_spectrum(2 * rows + 1, length, diffraction))
    even = phased(even, *cayley_spectrum(2 * rows + 2, length, diffraction))
    back_odd = jnp.einsum("...q,jq->...j", odd, odd_table, precision=HIGH)
    back_even = jnp.einsum("...q,jq->...j", even, even_table, precision=HIGH)
    return back_odd + back_even, back_odd - back_even


def shards(beam_field, region_labels, gain_table, diffraction, spectral_weight):
    block, spectra_dev, _, columns = beam_field.shape
    spectra = spectra_dev * lax.axis_size("wl")
    count = lax.axis_size("gx")
    me = lax.axis_index("gx")
    cells = block * count
    regions = gain_table.shape[0]
    region_index = jnp.arange(regions, dtype=jnp.int32)
    base_gain = jnp.sum(
        jnp.where(
            region_labels[None] == region_index[:, None, None], gain_table[:, None, None], 0.0
        ),
        axis=0,
    )

    def power_sum(values):
        return jnp.sum(spectral_weight[None, :, None, None] * (values * values), axis=(1, 2))

    fluence_in, counter = butterfly_sum(
        power_sum(beam_field), "wl", jnp.arange(columns, dtype=jnp.int32)
    )
    gain_in = base_gain / (1.0 + fluence_in / spectra)
    growth = jnp.exp(0.5 * gain_in)
    field = jnp.transpose(beam_field, (0, 2, 1, 3))
    in_order = Layout(major_to_minor=(0, 1, 2, 3))
    if columns % 2:
        amplified = with_layout_constraint(field * growth[:, None, None, :], in_order)
    else:
        half = columns // 2
        low = field[..., :half] * growth[:, None, None, :half]
        high = jnp.flip(field[..., half:], -1) * jnp.flip(growth[:, half:], -1)[:, None, None, :]
        amplified = (
            with_layout_constraint(low + high, in_order),
            with_layout_constraint(low - high, in_order),
        )

    factor_re, factor_im = inverse_factor(cells, diffraction)
    start = me * block
    around = start - 1 + jnp.arange(block + 2, dtype=jnp.int32)
    around_table = sine_rows(around, cells)
    green_re = jnp.einsum(
        "an,wn,bn->wab", around_table, factor_re, around_table, precision=HIGHEST
    )
    green_im = jnp.einsum(
        "an,wn,bn->wab", around_table, factor_im, around_table, precision=HIGHEST
    )

    def apply_block(rows_re, rows_im, values):
        kernel = jnp.stack(
            [
                jnp.stack([rows_re, -rows_im], axis=2),
                jnp.stack([rows_im, rows_re], axis=2),
            ],
            axis=1,
        )
        return jnp.einsum("wdack,kcwy->adwy", kernel, values, precision=HIGH)

    block_index = jnp.arange(count, dtype=jnp.int32)
    starts = block_index * block
    ends = starts + block - 1
    rise_re, rise_im = safe_ratio(
        *green_entries(starts + block, starts - 1, factor_re, factor_im, cells),
        *green_entries(starts, starts - 1, factor_re, factor_im, cells),
    )
    fall_re, fall_im = safe_ratio(
        *green_entries(ends - block, ends + 1, factor_re, factor_im, cells),
        *green_entries(ends, ends + 1, factor_re, factor_im, cells),
    )

    def span_product(ratio_re, ratio_im, first, length):
        total_re = jnp.ones_like(ratio_re[:, 0])
        total_im = jnp.zeros_like(ratio_im[:, 0])
        for offset in range(length):
            pick = jnp.clip(first + offset, 0, count - 1)
            total_re, total_im = complex_multiply(
                total_re, total_im, ratio_re[:, pick], ratio_im[:, pick]
            )
        return total_re[None, :, None], total_im[None, :, None]

    def scale(gain, values):
        moved = complex_multiply(gain[0], gain[1], values[0:1], values[1:2])
        return jnp.concatenate(moved, axis=0)

    first, second = cayley_rows(amplified, diffraction, counter)

    def joined(values, reversed_half):
        if reversed_half is None:
            return values
        return jnp.concatenate([values, jnp.flip(reversed_half, -1)], axis=-1)

    edge_re = jnp.concatenate([green_re[:, 0:1, 1 : block + 1], green_re[:, block + 1 :, 1 : block + 1]], axis=1)
    edge_im = jnp.concatenate([green_im[:, 0:1, 1 : block + 1], green_im[:, block + 1 :, 1 : block + 1]], axis=1)
    edges = joined(
        apply_block(edge_re, edge_im, first),
        None if second is None else apply_block(edge_re, edge_im, second),
    )
    along_y = joined(first, second)
    from_left = shifted(edges[1], "gx", 1)
    from_right = shifted(edges[0], "gx", -1)
    span = 1
    while span < count - 1:
        far_left = shifted(from_left, "gx", span)
        far_right = shifted(from_right, "gx", -span)
        from_left = from_left + scale(span_product(rise_re, rise_im, me - span, span), far_left)
        from_right = from_right + scale(span_product(fall_re, fall_im, me + 1, span), far_right)
        span *= 2

    local = apply_block(
        green_re[:, 1 : block + 1, 1 : block + 1], green_im[:, 1 : block + 1, 1 : block + 1], along_y
    )
    lead_re, lead_im = safe_ratio(
        green_re[:, 1 : block + 1, 0],
        green_im[:, 1 : block + 1, 0],
        green_re[:, 1:2, 0],
        green_im[:, 1:2, 0],
    )
    trail_re, trail_im = safe_ratio(
        green_re[:, 1 : block + 1, block + 1],
        green_im[:, 1 : block + 1, block + 1],
        green_re[:, block : block + 1, block + 1],
        green_im[:, block : block + 1, block + 1],
    )
    lead = complex_multiply(
        lead_re.T[:, :, None], lead_im.T[:, :, None], from_left[None, 0], from_left[None, 1]
    )
    trail = complex_multiply(
        trail_re.T[:, :, None], trail_im.T[:, :, None], from_right[None, 0], from_right[None, 1]
    )
    solved = local + jnp.stack([lead[0] + trail[0], lead[1] + trail[1]], axis=1)
    result = jnp.transpose(2.0 * solved - along_y, (0, 2, 1, 3))

    fluence_out, _ = butterfly_sum(power_sum(result), "wl", ())
    gain_out = base_gain / (1.0 + fluence_out / spectra)
    return (result * jnp.exp(0.5 * gain_out)[:, None, None, :], gain_out)


def solution(mesh):
    placed = (P("gx", "wl", None, None), P("gx", None), P(), P("wl"), P("wl"))
    return jax.shard_map(
        shards,
        mesh=mesh,
        in_specs=placed,
        out_specs=(P("gx", "wl", None, None), P("gx", None)),
        check_vma=False,
    )
```

```python
import math

import jax
import jax.numpy as jnp
from jax import lax
from jax.experimental.layout import Layout, with_layout_constraint
from jax.sharding import PartitionSpec as P

HIGHEST = lax.Precision.HIGHEST
HIGH = lax.Precision.HIGH


def complex_multiply(left_re, left_im, right_re, right_im):
    return (left_re * right_re - left_im * right_im, left_re * right_im + left_im * right_re)


def complex_div(top_re, top_im, bottom_re, bottom_im):
    magnitude = bottom_re * bottom_re + bottom_im * bottom_im
    return (
        (top_re * bottom_re + top_im * bottom_im) / magnitude,
        (top_im * bottom_re - top_re * bottom_im) / magnitude,
    )


def sine_rows(index, length):
    mode = jnp.arange(1, length + 1, dtype=jnp.int32)
    product = ((index + 1)[:, None] * mode[None, :]) % (2 * (length + 1))
    value = jnp.sin(product.astype(jnp.float32) * (math.pi / (length + 1))) * math.sqrt(
        2.0 / (length + 1)
    )
    inside = ((index >= 0) & (index < length))[:, None]
    return jnp.where(inside, value, 0.0)


def eigen_scaled(length, diffraction):
    counter = jnp.arange(1, length + 1, dtype=jnp.float32)
    eigenvalue = 4.0 * jnp.sin(counter * (math.pi / (2 * (length + 1)))) ** 2
    return diffraction[:, None] * eigenvalue[None, :]


def inverse_factor(length, diffraction):
    scaled = eigen_scaled(length, diffraction)
    magnitude = 1.0 + scaled * scaled
    return 1.0 / magnitude, -scaled / magnitude


def butterfly_sum(value, axis, rider):
    count = lax.axis_size(axis)
    if count & (count - 1):
        return lax.optimization_barrier((lax.psum(value, axis), rider))
    step = 1
    while step < count:
        pairs = [(i, i ^ step) for i in range(count)]
        value = value + lax.ppermute(value, axis, pairs)
        if step == 1:
            value, rider = lax.optimization_barrier((value, rider))
        step *= 2
    return value, rider


def shifted(value, axis, offset):
    count = lax.axis_size(axis)
    pairs = [(i, i + offset) for i in range(count) if 0 <= i + offset < count]
    return jax.tree.map(lambda part: lax.ppermute(part, axis, pairs), value)


def green_entries(rows, cols, factor_re, factor_im, length):
    row_table = sine_rows(rows, length)
    col_table = sine_rows(cols, length)
    both = row_table * col_table
    return (
        jnp.einsum("mn,wn->wm", both, factor_re, precision=HIGHEST),
        jnp.einsum("mn,wn->wm", both, factor_im, precision=HIGHEST),
    )


def safe_ratio(top_re, top_im, bottom_re, bottom_im):
    empty = (bottom_re == 0.0) & (bottom_im == 0.0)
    ratio_re, ratio_im = complex_div(
        top_re, top_im, jnp.where(empty, 1.0, bottom_re), bottom_im
    )
    return jnp.where(empty, 0.0, ratio_re), jnp.where(empty, 0.0, ratio_im)


def mode_sines(rows, modes, length):
    product = ((rows + 1)[:, None] * modes[None, :]) % (2 * (length + 1))
    return jnp.sin(product.astype(jnp.float32) * (math.pi / (length + 1))) * math.sqrt(
        2.0 / (length + 1)
    )


def cayley_spectrum(modes, length, diffraction):
    eigenvalue = 4.0 * jnp.sin(modes.astype(jnp.float32) * (math.pi / (2 * (length + 1)))) ** 2
    scaled = diffraction[:, None] * eigenvalue[None, :]
    magnitude = 1.0 + scaled * scaled
    return (1.0 - scaled * scaled) / magnitude, -2.0 * scaled / magnitude


def phased(spectrum, phase_re, phase_im):
    mixed_re, mixed_im = complex_multiply(
        spectrum[..., 0, :, :], spectrum[..., 1, :, :], phase_re, phase_im
    )
    return jnp.stack([mixed_re, mixed_im], axis=-3)


def cayley_rows(values, diffraction, counter):
    length = values.shape[-1]
    if length % 2:
        table = mode_sines(counter, counter + 1, length)
        phase = cayley_spectrum(counter + 1, length, diffraction)
        spectrum = jnp.dot(values, table, precision=HIGH)
        return jnp.dot(phased(spectrum, *phase), table, precision=HIGH), None
    half = length // 2
    rows = counter[:half]
    odd_table = mode_sines(rows, 2 * rows + 1, length)
    even_table = mode_sines(rows, 2 * rows + 2, length)
    low = values[..., :half]
    high = jnp.flip(values[..., half:], -1)
    odd = jnp.dot(low + high, odd_table, precision=HIGH)
    even = jnp.dot(low - high, even_table, precision=HIGH)
    odd = phased(odd, *cayley_spectrum(2 * rows + 1, length, diffraction))
    even = phased(even, *cayley_spectrum(2 * rows + 2, length, diffraction))
    back_odd = jnp.einsum("...q,jq->...j", odd, odd_table, precision=HIGH)
    back_even = jnp.einsum("...q,jq->...j", even, even_table, precision=HIGH)
    return back_odd + back_even, back_odd - back_even


def shards(beam_field, region_labels, gain_table, diffraction, spectral_weight):
    block, spectra_dev, _, columns = beam_field.shape
    spectra = spectra_dev * lax.axis_size("wl")
    count = lax.axis_size("gx")
    me = lax.axis_index("gx")
    cells = block * count
    regions = gain_table.shape[0]
    region_index = jnp.arange(regions, dtype=jnp.int32)
    base_gain = jnp.sum(
        jnp.where(
            region_labels[None] == region_index[:, None, None], gain_table[:, None, None], 0.0
        ),
        axis=0,
    )

    def power_sum(values):
        return jnp.sum(spectral_weight[None, :, None, None] * (values * values), axis=(1, 2))

    fluence_in, (counter, offsets) = butterfly_sum(
        power_sum(beam_field),
        "wl",
        (jnp.arange(columns, dtype=jnp.int32), jnp.arange(block + 2, dtype=jnp.int32)),
    )
    gain_in = base_gain / (1.0 + fluence_in / spectra)
    amplified = with_layout_constraint(
        jnp.transpose(beam_field, (0, 2, 1, 3)) * jnp.exp(0.5 * gain_in)[:, None, None, :],
        Layout(major_to_minor=(0, 1, 2, 3)),
    )

    factor_re, factor_im = inverse_factor(cells, diffraction)
    start = me * block
    around = start - 1 + offsets
    around_table = sine_rows(around, cells)
    green_re = jnp.einsum(
        "an,wn,bn->wab", around_table, factor_re, around_table, precision=HIGHEST
    )
    green_im = jnp.einsum(
        "an,wn,bn->wab", around_table, factor_im, around_table, precision=HIGHEST
    )

    def apply_block(rows_re, rows_im, values):
        kernel = jnp.stack(
            [
                jnp.stack([rows_re, -rows_im], axis=2),
                jnp.stack([rows_im, rows_re], axis=2),
            ],
            axis=1,
        )
        return jnp.einsum("wdack,kcwy->adwy", kernel, values, precision=HIGH)

    block_index = jnp.arange(count, dtype=jnp.int32)
    starts = block_index * block
    ends = starts + block - 1
    rise_re, rise_im = safe_ratio(
        *green_entries(starts + block, starts - 1, factor_re, factor_im, cells),
        *green_entries(starts, starts - 1, factor_re, factor_im, cells),
    )
    fall_re, fall_im = safe_ratio(
        *green_entries(ends - block, ends + 1, factor_re, factor_im, cells),
        *green_entries(ends, ends + 1, factor_re, factor_im, cells),
    )

    def span_product(ratio_re, ratio_im, first, length):
        total_re = jnp.ones_like(ratio_re[:, 0])
        total_im = jnp.zeros_like(ratio_im[:, 0])
        for offset in range(length):
            pick = jnp.clip(first + offset, 0, count - 1)
            total_re, total_im = complex_multiply(
                total_re, total_im, ratio_re[:, pick], ratio_im[:, pick]
            )
        return total_re[None, :, None], total_im[None, :, None]

    def scale(gain, values):
        moved = complex_multiply(gain[0], gain[1], values[0:1], values[1:2])
        return jnp.concatenate(moved, axis=0)

    first, second = cayley_rows(amplified, diffraction, counter)

    def joined(values, reversed_half):
        if reversed_half is None:
            return values
        return jnp.concatenate([values, jnp.flip(reversed_half, -1)], axis=-1)

    edge_re = jnp.concatenate([green_re[:, 0:1, 1 : block + 1], green_re[:, block + 1 :, 1 : block + 1]], axis=1)
    edge_im = jnp.concatenate([green_im[:, 0:1, 1 : block + 1], green_im[:, block + 1 :, 1 : block + 1]], axis=1)
    edges = joined(
        apply_block(edge_re, edge_im, first),
        None if second is None else apply_block(edge_re, edge_im, second),
    )
    along_y = joined(first, second)
    from_left = shifted(edges[1], "gx", 1)
    from_right = shifted(edges[0], "gx", -1)
    span = 1
    while span < count - 1:
        far_left = shifted(from_left, "gx", span)
        far_right = shifted(from_right, "gx", -span)
        from_left = from_left + scale(span_product(rise_re, rise_im, me - span, span), far_left)
        from_right = from_right + scale(span_product(fall_re, fall_im, me + 1, span), far_right)
        span *= 2

    local = apply_block(
        green_re[:, 1 : block + 1, 1 : block + 1], green_im[:, 1 : block + 1, 1 : block + 1], along_y
    )
    lead_re, lead_im = safe_ratio(
        green_re[:, 1 : block + 1, 0],
        green_im[:, 1 : block + 1, 0],
        green_re[:, 1:2, 0],
        green_im[:, 1:2, 0],
    )
    trail_re, trail_im = safe_ratio(
        green_re[:, 1 : block + 1, block + 1],
        green_im[:, 1 : block + 1, block + 1],
        green_re[:, block : block + 1, block + 1],
        green_im[:, block : block + 1, block + 1],
    )
    lead = complex_multiply(
        lead_re.T[:, :, None], lead_im.T[:, :, None], from_left[None, 0], from_left[None, 1]
    )
    trail = complex_multiply(
        trail_re.T[:, :, None], trail_im.T[:, :, None], from_right[None, 0], from_right[None, 1]
    )
    solved = local + jnp.stack([lead[0] + trail[0], lead[1] + trail[1]], axis=1)
    result = jnp.transpose(2.0 * solved - along_y, (0, 2, 1, 3))

    fluence_out, _ = butterfly_sum(power_sum(result), "wl", ())
    gain_out = base_gain / (1.0 + fluence_out / spectra)
    return (result * jnp.exp(0.5 * gain_out)[:, None, None, :], gain_out)


def solution(mesh):
    placed = (P("gx", "wl", None, None), P("gx", None), P(), P("wl"), P("wl"))
    return jax.shard_map(
        shards,
        mesh=mesh,
        in_specs=placed,
        out_specs=(P("gx", "wl", None, None), P("gx", None)),
        check_vma=False,
    )
```

```python
import math

import jax
import jax.numpy as jnp
from jax import lax
from jax.experimental.layout import Layout, with_layout_constraint
from jax.sharding import PartitionSpec as P

HIGHEST = lax.Precision.HIGHEST
HIGH = lax.Precision.HIGH


def complex_multiply(left_re, left_im, right_re, right_im):
    return (left_re * right_re - left_im * right_im, left_re * right_im + left_im * right_re)


def complex_div(top_re, top_im, bottom_re, bottom_im):
    magnitude = bottom_re * bottom_re + bottom_im * bottom_im
    return (
        (top_re * bottom_re + top_im * bottom_im) / magnitude,
        (top_im * bottom_re - top_re * bottom_im) / magnitude,
    )


def sine_rows(index, length):
    mode = jnp.arange(1, length + 1, dtype=jnp.int32)
    product = ((index + 1)[:, None] * mode[None, :]) % (2 * (length + 1))
    value = jnp.sin(product.astype(jnp.float32) * (math.pi / (length + 1))) * math.sqrt(
        2.0 / (length + 1)
    )
    inside = ((index >= 0) & (index < length))[:, None]
    return jnp.where(inside, value, 0.0)


def eigen_scaled(length, diffraction):
    counter = jnp.arange(1, length + 1, dtype=jnp.float32)
    eigenvalue = 4.0 * jnp.sin(counter * (math.pi / (2 * (length + 1)))) ** 2
    return diffraction[:, None] * eigenvalue[None, :]


def inverse_factor(length, diffraction):
    scaled = eigen_scaled(length, diffraction)
    magnitude = 1.0 + scaled * scaled
    return 1.0 / magnitude, -scaled / magnitude


def butterfly_sum(value, axis, rider):
    count = lax.axis_size(axis)
    if count & (count - 1):
        return lax.optimization_barrier((lax.psum(value, axis), rider))
    step = 1
    while step < count:
        pairs = [(i, i ^ step) for i in range(count)]
        value = value + lax.ppermute(value, axis, pairs)
        if step == 1:
            value, rider = lax.optimization_barrier((value, rider))
        step *= 2
    return value, rider


def shifted(value, axis, offset):
    count = lax.axis_size(axis)
    pairs = [(i, i + offset) for i in range(count) if 0 <= i + offset < count]
    return jax.tree.map(lambda part: lax.ppermute(part, axis, pairs), value)


def green_entries(rows, cols, factor_re, factor_im, length):
    row_table = sine_rows(rows, length)
    col_table = sine_rows(cols, length)
    both = row_table * col_table
    return (
        jnp.einsum("mn,wn->wm", both, factor_re, precision=HIGHEST),
        jnp.einsum("mn,wn->wm", both, factor_im, precision=HIGHEST),
    )


def safe_ratio(top_re, top_im, bottom_re, bottom_im):
    empty = (bottom_re == 0.0) & (bottom_im == 0.0)
    ratio_re, ratio_im = complex_div(
        top_re, top_im, jnp.where(empty, 1.0, bottom_re), bottom_im
    )
    return jnp.where(empty, 0.0, ratio_re), jnp.where(empty, 0.0, ratio_im)


def mode_sines(rows, modes, length):
    product = ((rows + 1)[:, None] * modes[None, :]) % (2 * (length + 1))
    return jnp.sin(product.astype(jnp.float32) * (math.pi / (length + 1))) * math.sqrt(
        2.0 / (length + 1)
    )


def cayley_spectrum(modes, length, diffraction):
    eigenvalue = 4.0 * jnp.sin(modes.astype(jnp.float32) * (math.pi / (2 * (length + 1)))) ** 2
    scaled = diffraction[:, None] * eigenvalue[None, :]
    magnitude = 1.0 + scaled * scaled
    return (1.0 - scaled * scaled) / magnitude, -2.0 * scaled / magnitude


def phased(spectrum, phase_re, phase_im):
    mixed_re, mixed_im = complex_multiply(
        spectrum[..., 0, :, :], spectrum[..., 1, :, :], phase_re, phase_im
    )
    return jnp.stack([mixed_re, mixed_im], axis=-3)


def cayley_rows(values, diffraction, counter):
    length = values.shape[-1]
    if length % 2:
        table = mode_sines(counter, counter + 1, length)
        phase = cayley_spectrum(counter + 1, length, diffraction)
        spectrum = jnp.dot(values, table, precision=HIGH)
        return jnp.dot(phased(spectrum, *phase), table, precision=HIGH), None
    half = length // 2
    rows = counter[:half]
    odd_table = mode_sines(rows, 2 * rows + 1, length)
    even_table = mode_sines(rows, 2 * rows + 2, length)
    low = values[..., :half]
    high = jnp.flip(values[..., half:], -1)
    odd = jnp.dot(low + high, odd_table, precision=HIGH)
    even = jnp.dot(low - high, even_table, precision=HIGH)
    odd = phased(odd, *cayley_spectrum(2 * rows + 1, length, diffraction))
    even = phased(even, *cayley_spectrum(2 * rows + 2, length, diffraction))
    back_odd = jnp.einsum("...q,jq->...j", odd, odd_table, precision=HIGH)
    back_even = jnp.einsum("...q,jq->...j", even, even_table, precision=HIGH)
    return back_odd + back_even, back_odd - back_even


def shards(beam_field, region_labels, gain_table, diffraction, spectral_weight):
    block, spectra_dev, _, columns = beam_field.shape
    spectra = spectra_dev * lax.axis_size("wl")
    count = lax.axis_size("gx")
    me = lax.axis_index("gx")
    cells = block * count
    regions = gain_table.shape[0]
    region_index = jnp.arange(regions, dtype=jnp.int32)
    base_gain = jnp.sum(
        jnp.where(
            region_labels[None] == region_index[:, None, None], gain_table[:, None, None], 0.0
        ),
        axis=0,
    )

    def power_sum(values):
        return jnp.sum(spectral_weight[None, :, None, None] * (values * values), axis=(1, 2))

    field = with_layout_constraint(
        jnp.transpose(beam_field, (0, 2, 1, 3)), Layout(major_to_minor=(0, 1, 2, 3))
    )
    fluence_in, counter = butterfly_sum(
        jnp.sum(spectral_weight[None, None, :, None] * (field * field), axis=(1, 2)),
        "wl",
        jnp.arange(columns, dtype=jnp.int32),
    )
    gain_in = base_gain / (1.0 + fluence_in / spectra)
    amplified = with_layout_constraint(
        field * jnp.exp(0.5 * gain_in)[:, None, None, :], Layout(major_to_minor=(0, 1, 2, 3))
    )

    factor_re, factor_im = inverse_factor(cells, diffraction)
    start = me * block
    around = start - 1 + jnp.arange(block + 2, dtype=jnp.int32)
    around_table = sine_rows(around, cells)
    green_re = jnp.einsum(
        "an,wn,bn->wab", around_table, factor_re, around_table, precision=HIGHEST
    )
    green_im = jnp.einsum(
        "an,wn,bn->wab", around_table, factor_im, around_table, precision=HIGHEST
    )

    def apply_block(rows_re, rows_im, values):
        kernel = jnp.stack(
            [
                jnp.stack([rows_re, -rows_im], axis=2),
                jnp.stack([rows_im, rows_re], axis=2),
            ],
            axis=1,
        )
        return jnp.einsum("wdack,kcwy->adwy", kernel, values, precision=HIGH)

    block_index = jnp.arange(count, dtype=jnp.int32)
    starts = block_index * block
    ends = starts + block - 1
    rise_re, rise_im = safe_ratio(
        *green_entries(starts + block, starts - 1, factor_re, factor_im, cells),
        *green_entries(starts, starts - 1, factor_re, factor_im, cells),
    )
    fall_re, fall_im = safe_ratio(
        *green_entries(ends - block, ends + 1, factor_re, factor_im, cells),
        *green_entries(ends, ends + 1, factor_re, factor_im, cells),
    )

    def span_product(ratio_re, ratio_im, first, length):
        total_re = jnp.ones_like(ratio_re[:, 0])
        total_im = jnp.zeros_like(ratio_im[:, 0])
        for offset in range(length):
            pick = jnp.clip(first + offset, 0, count - 1)
            total_re, total_im = complex_multiply(
                total_re, total_im, ratio_re[:, pick], ratio_im[:, pick]
            )
        return total_re[None, :, None], total_im[None, :, None]

    def scale(gain, values):
        moved = complex_multiply(gain[0], gain[1], values[0:1], values[1:2])
        return jnp.concatenate(moved, axis=0)

    first, second = cayley_rows(amplified, diffraction, counter)

    def joined(values, reversed_half):
        if reversed_half is None:
            return values
        return jnp.concatenate([values, jnp.flip(reversed_half, -1)], axis=-1)

    edge_re = jnp.concatenate([green_re[:, 0:1, 1 : block + 1], green_re[:, block + 1 :, 1 : block + 1]], axis=1)
    edge_im = jnp.concatenate([green_im[:, 0:1, 1 : block + 1], green_im[:, block + 1 :, 1 : block + 1]], axis=1)
    edges = joined(
        apply_block(edge_re, edge_im, first),
        None if second is None else apply_block(edge_re, edge_im, second),
    )
    along_y = joined(first, second)
    from_left = shifted(edges[1], "gx", 1)
    from_right = shifted(edges[0], "gx", -1)
    span = 1
    while span < count - 1:
        far_left = shifted(from_left, "gx", span)
        far_right = shifted(from_right, "gx", -span)
        from_left = from_left + scale(span_product(rise_re, rise_im, me - span, span), far_left)
        from_right = from_right + scale(span_product(fall_re, fall_im, me + 1, span), far_right)
        span *= 2

    local = apply_block(
        green_re[:, 1 : block + 1, 1 : block + 1], green_im[:, 1 : block + 1, 1 : block + 1], along_y
    )
    lead_re, lead_im = safe_ratio(
        green_re[:, 1 : block + 1, 0],
        green_im[:, 1 : block + 1, 0],
        green_re[:, 1:2, 0],
        green_im[:, 1:2, 0],
    )
    trail_re, trail_im = safe_ratio(
        green_re[:, 1 : block + 1, block + 1],
        green_im[:, 1 : block + 1, block + 1],
        green_re[:, block : block + 1, block + 1],
        green_im[:, block : block + 1, block + 1],
    )
    lead = complex_multiply(
        lead_re.T[:, :, None], lead_im.T[:, :, None], from_left[None, 0], from_left[None, 1]
    )
    trail = complex_multiply(
        trail_re.T[:, :, None], trail_im.T[:, :, None], from_right[None, 0], from_right[None, 1]
    )
    solved = local + jnp.stack([lead[0] + trail[0], lead[1] + trail[1]], axis=1)
    result = jnp.transpose(2.0 * solved - along_y, (0, 2, 1, 3))

    fluence_out, _ = butterfly_sum(power_sum(result), "wl", ())
    gain_out = base_gain / (1.0 + fluence_out / spectra)
    return (result * jnp.exp(0.5 * gain_out)[:, None, None, :], gain_out)


def solution(mesh):
    placed = (P("gx", "wl", None, None), P("gx", None), P(), P("wl"), P("wl"))
    return jax.shard_map(
        shards,
        mesh=mesh,
        in_specs=placed,
        out_specs=(P("gx", "wl", None, None), P("gx", None)),
        check_vma=False,
    )
```

```python
import math

import jax
import jax.numpy as jnp
from jax import lax
from jax.experimental.layout import Layout, with_layout_constraint
from jax.sharding import PartitionSpec as P

HIGHEST = lax.Precision.HIGHEST
HIGH = lax.Precision.HIGH


def complex_multiply(left_re, left_im, right_re, right_im):
    return (left_re * right_re - left_im * right_im, left_re * right_im + left_im * right_re)


def complex_div(top_re, top_im, bottom_re, bottom_im):
    magnitude = bottom_re * bottom_re + bottom_im * bottom_im
    return (
        (top_re * bottom_re + top_im * bottom_im) / magnitude,
        (top_im * bottom_re - top_re * bottom_im) / magnitude,
    )


def sine_rows(index, length):
    mode = jnp.arange(1, length + 1, dtype=jnp.int32)
    product = ((index + 1)[:, None] * mode[None, :]) % (2 * (length + 1))
    value = jnp.sin(product.astype(jnp.float32) * (math.pi / (length + 1))) * math.sqrt(
        2.0 / (length + 1)
    )
    inside = ((index >= 0) & (index < length))[:, None]
    return jnp.where(inside, value, 0.0)


def eigen_scaled(length, diffraction):
    counter = jnp.arange(1, length + 1, dtype=jnp.float32)
    eigenvalue = 4.0 * jnp.sin(counter * (math.pi / (2 * (length + 1)))) ** 2
    return diffraction[:, None] * eigenvalue[None, :]


def inverse_factor(length, diffraction):
    scaled = eigen_scaled(length, diffraction)
    magnitude = 1.0 + scaled * scaled
    return 1.0 / magnitude, -scaled / magnitude


def butterfly_sum(value, axis, rider):
    count = lax.axis_size(axis)
    if count & (count - 1):
        return lax.optimization_barrier((lax.psum(value, axis), rider))
    if count <= 4:
        me = lax.axis_index(axis)
        parts = [value] + [
            lax.ppermute(value, axis, [(i, i ^ k) for i in range(count)]) for k in range(1, count)
        ]
        total = None
        for source in range(count):
            term = parts[0]
            for k in range(1, count):
                term = jnp.where(jnp.bitwise_xor(me, source) == k, parts[k], term)
            total = term if total is None else total + term
        return lax.optimization_barrier((total, rider))
    step = 1
    while step < count:
        pairs = [(i, i ^ step) for i in range(count)]
        value = value + lax.ppermute(value, axis, pairs)
        if step == 1:
            value, rider = lax.optimization_barrier((value, rider))
        step *= 2
    return value, rider


def shifted(value, axis, offset):
    count = lax.axis_size(axis)
    pairs = [(i, i + offset) for i in range(count) if 0 <= i + offset < count]
    return jax.tree.map(lambda part: lax.ppermute(part, axis, pairs), value)


def green_entries(rows, cols, factor_re, factor_im, length):
    row_table = sine_rows(rows, length)
    col_table = sine_rows(cols, length)
    both = row_table * col_table
    return (
        jnp.einsum("mn,wn->wm", both, factor_re, precision=HIGHEST),
        jnp.einsum("mn,wn->wm", both, factor_im, precision=HIGHEST),
    )


def safe_ratio(top_re, top_im, bottom_re, bottom_im):
    empty = (bottom_re == 0.0) & (bottom_im == 0.0)
    ratio_re, ratio_im = complex_div(
        top_re, top_im, jnp.where(empty, 1.0, bottom_re), bottom_im
    )
    return jnp.where(empty, 0.0, ratio_re), jnp.where(empty, 0.0, ratio_im)


def mode_sines(rows, modes, length):
    product = ((rows + 1)[:, None] * modes[None, :]) % (2 * (length + 1))
    return jnp.sin(product.astype(jnp.float32) * (math.pi / (length + 1))) * math.sqrt(
        2.0 / (length + 1)
    )


def cayley_spectrum(modes, length, diffraction):
    eigenvalue = 4.0 * jnp.sin(modes.astype(jnp.float32) * (math.pi / (2 * (length + 1)))) ** 2
    scaled = diffraction[:, None] * eigenvalue[None, :]
    magnitude = 1.0 + scaled * scaled
    return (1.0 - scaled * scaled) / magnitude, -2.0 * scaled / magnitude


def phased(spectrum, phase_re, phase_im):
    mixed_re, mixed_im = complex_multiply(
        spectrum[..., 0, :, :], spectrum[..., 1, :, :], phase_re, phase_im
    )
    return jnp.stack([mixed_re, mixed_im], axis=-3)


def cayley_rows(values, diffraction, counter):
    length = values.shape[-1]
    if length % 2:
        table = mode_sines(counter, counter + 1, length)
        phase = cayley_spectrum(counter + 1, length, diffraction)
        spectrum = jnp.dot(values, table, precision=HIGH)
        return jnp.dot(phased(spectrum, *phase), table, precision=HIGH), None
    half = length // 2
    rows = counter[:half]
    odd_table = mode_sines(rows, 2 * rows + 1, length)
    even_table = mode_sines(rows, 2 * rows + 2, length)
    low = values[..., :half]
    high = jnp.flip(values[..., half:], -1)
    odd = jnp.dot(low + high, odd_table, precision=HIGH)
    even = jnp.dot(low - high, even_table, precision=HIGH)
    odd = phased(odd, *cayley_spectrum(2 * rows + 1, length, diffraction))
    even = phased(even, *cayley_spectrum(2 * rows + 2, length, diffraction))
    back_odd = jnp.einsum("...q,jq->...j", odd, odd_table, precision=HIGH)
    back_even = jnp.einsum("...q,jq->...j", even, even_table, precision=HIGH)
    return back_odd + back_even, back_odd - back_even


def shards(beam_field, region_labels, gain_table, diffraction, spectral_weight):
    block, spectra_dev, _, columns = beam_field.shape
    spectra = spectra_dev * lax.axis_size("wl")
    count = lax.axis_size("gx")
    me = lax.axis_index("gx")
    cells = block * count
    regions = gain_table.shape[0]
    region_index = jnp.arange(regions, dtype=jnp.int32)
    base_gain = jnp.sum(
        jnp.where(
            region_labels[None] == region_index[:, None, None], gain_table[:, None, None], 0.0
        ),
        axis=0,
    )

    def power_sum(values):
        return jnp.sum(spectral_weight[None, :, None, None] * (values * values), axis=(1, 2))

    fluence_in, counter = butterfly_sum(
        power_sum(beam_field), "wl", jnp.arange(columns, dtype=jnp.int32)
    )
    gain_in = base_gain / (1.0 + fluence_in / spectra)
    amplified = with_layout_constraint(
        jnp.transpose(beam_field, (0, 2, 1, 3)) * jnp.exp(0.5 * gain_in)[:, None, None, :],
        Layout(major_to_minor=(0, 1, 2, 3)),
    )

    factor_re, factor_im = inverse_factor(cells, diffraction)
    start = me * block
    around = start - 1 + jnp.arange(block + 2, dtype=jnp.int32)
    around_table = sine_rows(around, cells)
    green_re = jnp.einsum(
        "an,wn,bn->wab", around_table, factor_re, around_table, precision=HIGHEST
    )
    green_im = jnp.einsum(
        "an,wn,bn->wab", around_table, factor_im, around_table, precision=HIGHEST
    )

    def apply_block(rows_re, rows_im, values):
        kernel = jnp.stack(
            [
                jnp.stack([rows_re, -rows_im], axis=2),
                jnp.stack([rows_im, rows_re], axis=2),
            ],
            axis=1,
        )
        return jnp.einsum("wdack,kcwy->adwy", kernel, values, precision=HIGH)

    block_index = jnp.arange(count, dtype=jnp.int32)
    starts = block_index * block
    ends = starts + block - 1
    rise_re, rise_im = safe_ratio(
        *green_entries(starts + block, starts - 1, factor_re, factor_im, cells),
        *green_entries(starts, starts - 1, factor_re, factor_im, cells),
    )
    fall_re, fall_im = safe_ratio(
        *green_entries(ends - block, ends + 1, factor_re, factor_im, cells),
        *green_entries(ends, ends + 1, factor_re, factor_im, cells),
    )

    def span_product(ratio_re, ratio_im, first, length):
        total_re = jnp.ones_like(ratio_re[:, 0])
        total_im = jnp.zeros_like(ratio_im[:, 0])
        for offset in range(length):
            pick = jnp.clip(first + offset, 0, count - 1)
            total_re, total_im = complex_multiply(
                total_re, total_im, ratio_re[:, pick], ratio_im[:, pick]
            )
        return total_re[None, :, None], total_im[None, :, None]

    def scale(gain, values):
        moved = complex_multiply(gain[0], gain[1], values[0:1], values[1:2])
        return jnp.concatenate(moved, axis=0)

    first, second = cayley_rows(amplified, diffraction, counter)

    def joined(values, reversed_half):
        if reversed_half is None:
            return values
        return jnp.concatenate([values, jnp.flip(reversed_half, -1)], axis=-1)

    edge_re = jnp.concatenate([green_re[:, 0:1, 1 : block + 1], green_re[:, block + 1 :, 1 : block + 1]], axis=1)
    edge_im = jnp.concatenate([green_im[:, 0:1, 1 : block + 1], green_im[:, block + 1 :, 1 : block + 1]], axis=1)
    edges = joined(
        apply_block(edge_re, edge_im, first),
        None if second is None else apply_block(edge_re, edge_im, second),
    )
    along_y = joined(first, second)
    from_left = shifted(edges[1], "gx", 1)
    from_right = shifted(edges[0], "gx", -1)
    span = 1
    while span < count - 1:
        far_left = shifted(from_left, "gx", span)
        far_right = shifted(from_right, "gx", -span)
        from_left = from_left + scale(span_product(rise_re, rise_im, me - span, span), far_left)
        from_right = from_right + scale(span_product(fall_re, fall_im, me + 1, span), far_right)
        span *= 2

    local = apply_block(
        green_re[:, 1 : block + 1, 1 : block + 1], green_im[:, 1 : block + 1, 1 : block + 1], along_y
    )
    lead_re, lead_im = safe_ratio(
        green_re[:, 1 : block + 1, 0],
        green_im[:, 1 : block + 1, 0],
        green_re[:, 1:2, 0],
        green_im[:, 1:2, 0],
    )
    trail_re, trail_im = safe_ratio(
        green_re[:, 1 : block + 1, block + 1],
        green_im[:, 1 : block + 1, block + 1],
        green_re[:, block : block + 1, block + 1],
        green_im[:, block : block + 1, block + 1],
    )
    lead = complex_multiply(
        lead_re.T[:, :, None], lead_im.T[:, :, None], from_left[None, 0], from_left[None, 1]
    )
    trail = complex_multiply(
        trail_re.T[:, :, None], trail_im.T[:, :, None], from_right[None, 0], from_right[None, 1]
    )
    solved = local + jnp.stack([lead[0] + trail[0], lead[1] + trail[1]], axis=1)
    result = jnp.transpose(2.0 * solved - along_y, (0, 2, 1, 3))

    fluence_out, _ = butterfly_sum(power_sum(result), "wl", ())
    gain_out = base_gain / (1.0 + fluence_out / spectra)
    return (result * jnp.exp(0.5 * gain_out)[:, None, None, :], gain_out)


def solution(mesh):
    placed = (P("gx", "wl", None, None), P("gx", None), P(), P("wl"), P("wl"))
    return jax.shard_map(
        shards,
        mesh=mesh,
        in_specs=placed,
        out_specs=(P("gx", "wl", None, None), P("gx", None)),
        check_vma=False,
    )
```

```python
import math

import jax
import jax.numpy as jnp
from jax import lax
from jax.experimental.layout import Layout, with_layout_constraint
from jax.sharding import PartitionSpec as P

HIGHEST = lax.Precision.HIGHEST
HIGH = lax.Precision.HIGH


def complex_multiply(left_re, left_im, right_re, right_im):
    return (left_re * right_re - left_im * right_im, left_re * right_im + left_im * right_re)


def complex_div(top_re, top_im, bottom_re, bottom_im):
    magnitude = bottom_re * bottom_re + bottom_im * bottom_im
    return (
        (top_re * bottom_re + top_im * bottom_im) / magnitude,
        (top_im * bottom_re - top_re * bottom_im) / magnitude,
    )


def sine_rows(index, length):
    mode = jnp.arange(1, length + 1, dtype=jnp.int32)
    product = ((index + 1)[:, None] * mode[None, :]) % (2 * (length + 1))
    value = jnp.sin(product.astype(jnp.float32) * (math.pi / (length + 1))) * math.sqrt(
        2.0 / (length + 1)
    )
    inside = ((index >= 0) & (index < length))[:, None]
    return jnp.where(inside, value, 0.0)


def eigen_scaled(length, diffraction):
    counter = jnp.arange(1, length + 1, dtype=jnp.float32)
    eigenvalue = 4.0 * jnp.sin(counter * (math.pi / (2 * (length + 1)))) ** 2
    return diffraction[:, None] * eigenvalue[None, :]


def inverse_factor(length, diffraction):
    scaled = eigen_scaled(length, diffraction)
    magnitude = 1.0 + scaled * scaled
    return 1.0 / magnitude, -scaled / magnitude


def butterfly_sum(value, axis, rider):
    count = lax.axis_size(axis)
    if count & (count - 1):
        return lax.optimization_barrier((lax.psum(value, axis), rider))
    step = 1
    while step < count:
        pairs = [(i, i ^ step) for i in range(count)]
        value = value + lax.ppermute(value, axis, pairs)
        if step == 1:
            value, rider = lax.optimization_barrier((value, rider))
        step *= 2
    return value, rider


def shifted(value, axis, offset):
    count = lax.axis_size(axis)
    pairs = [(i, i + offset) for i in range(count) if 0 <= i + offset < count]
    return jax.tree.map(lambda part: lax.ppermute(part, axis, pairs), value)


def green_entries(rows, cols, factor_re, factor_im, length):
    row_table = sine_rows(rows, length)
    col_table = sine_rows(cols, length)
    both = row_table * col_table
    return (
        jnp.einsum("mn,wn->wm", both, factor_re, precision=HIGHEST),
        jnp.einsum("mn,wn->wm", both, factor_im, precision=HIGHEST),
    )


def safe_ratio(top_re, top_im, bottom_re, bottom_im):
    empty = (bottom_re == 0.0) & (bottom_im == 0.0)
    ratio_re, ratio_im = complex_div(
        top_re, top_im, jnp.where(empty, 1.0, bottom_re), bottom_im
    )
    return jnp.where(empty, 0.0, ratio_re), jnp.where(empty, 0.0, ratio_im)


def mode_sines(rows, modes, length):
    product = ((rows + 1)[:, None] * modes[None, :]) % (2 * (length + 1))
    return jnp.sin(product.astype(jnp.float32) * (math.pi / (length + 1))) * math.sqrt(
        2.0 / (length + 1)
    )


def cayley_spectrum(modes, length, diffraction):
    eigenvalue = 4.0 * jnp.sin(modes.astype(jnp.float32) * (math.pi / (2 * (length + 1)))) ** 2
    scaled = diffraction[:, None] * eigenvalue[None, :]
    magnitude = 1.0 + scaled * scaled
    return (1.0 - scaled * scaled) / magnitude, -2.0 * scaled / magnitude


def phased(spectrum, phase_re, phase_im):
    mixed_re, mixed_im = complex_multiply(
        spectrum[..., 0, :, :], spectrum[..., 1, :, :], phase_re, phase_im
    )
    return jnp.stack([mixed_re, mixed_im], axis=-3)


def cayley_rows(values, diffraction, counter):
    length = counter.shape[0]
    if length % 2:
        table = mode_sines(counter, counter + 1, length)
        phase = cayley_spectrum(counter + 1, length, diffraction)
        spectrum = jnp.dot(values, table, precision=HIGH)
        return jnp.dot(phased(spectrum, *phase), table, precision=HIGH), None
    half = length // 2
    rows = counter[:half]
    odd_table = mode_sines(rows, 2 * rows + 1, length)
    even_table = mode_sines(rows, 2 * rows + 2, length)
    low, high = values
    high = jnp.flip(high, -1)
    odd = jnp.dot(low + high, odd_table, precision=HIGH)
    even = jnp.dot(low - high, even_table, precision=HIGH)
    odd = phased(odd, *cayley_spectrum(2 * rows + 1, length, diffraction))
    even = phased(even, *cayley_spectrum(2 * rows + 2, length, diffraction))
    back_odd = jnp.einsum("...q,jq->...j", odd, odd_table, precision=HIGH)
    back_even = jnp.einsum("...q,jq->...j", even, even_table, precision=HIGH)
    return back_odd + back_even, back_odd - back_even


def shards(beam_field, region_labels, gain_table, diffraction, spectral_weight):
    block, spectra_dev, _, columns = beam_field.shape
    spectra = spectra_dev * lax.axis_size("wl")
    count = lax.axis_size("gx")
    me = lax.axis_index("gx")
    cells = block * count
    regions = gain_table.shape[0]
    region_index = jnp.arange(regions, dtype=jnp.int32)
    base_gain = jnp.sum(
        jnp.where(
            region_labels[None] == region_index[:, None, None], gain_table[:, None, None], 0.0
        ),
        axis=0,
    )

    def power_sum(values):
        return jnp.sum(spectral_weight[None, :, None, None] * (values * values), axis=(1, 2))

    fluence_in, counter = butterfly_sum(
        power_sum(beam_field), "wl", jnp.arange(columns, dtype=jnp.int32)
    )
    gain_in = base_gain / (1.0 + fluence_in / spectra)
    growth = jnp.exp(0.5 * gain_in)
    field = jnp.transpose(beam_field, (0, 2, 1, 3))
    in_order = Layout(major_to_minor=(0, 1, 2, 3))
    if columns % 2:
        amplified = with_layout_constraint(field * growth[:, None, None, :], in_order)
    else:
        half = columns // 2
        amplified = tuple(
            with_layout_constraint(field[..., part] * growth[:, None, None, part], in_order)
            for part in (slice(0, half), slice(half, columns))
        )

    factor_re, factor_im = inverse_factor(cells, diffraction)
    start = me * block
    around = start - 1 + jnp.arange(block + 2, dtype=jnp.int32)
    around_table = sine_rows(around, cells)
    green_re = jnp.einsum(
        "an,wn,bn->wab", around_table, factor_re, around_table, precision=HIGHEST
    )
    green_im = jnp.einsum(
        "an,wn,bn->wab", around_table, factor_im, around_table, precision=HIGHEST
    )

    def apply_block(rows_re, rows_im, values):
        kernel = jnp.stack(
            [
                jnp.stack([rows_re, -rows_im], axis=2),
                jnp.stack([rows_im, rows_re], axis=2),
            ],
            axis=1,
        )
        return jnp.einsum("wdack,kcwy->adwy", kernel, values, precision=HIGH)

    block_index = jnp.arange(count, dtype=jnp.int32)
    starts = block_index * block
    ends = starts + block - 1
    rise_re, rise_im = safe_ratio(
        *green_entries(starts + block, starts - 1, factor_re, factor_im, cells),
        *green_entries(starts, starts - 1, factor_re, factor_im, cells),
    )
    fall_re, fall_im = safe_ratio(
        *green_entries(ends - block, ends + 1, factor_re, factor_im, cells),
        *green_entries(ends, ends + 1, factor_re, factor_im, cells),
    )

    def span_product(ratio_re, ratio_im, first, length):
        total_re = jnp.ones_like(ratio_re[:, 0])
        total_im = jnp.zeros_like(ratio_im[:, 0])
        for offset in range(length):
            pick = jnp.clip(first + offset, 0, count - 1)
            total_re, total_im = complex_multiply(
                total_re, total_im, ratio_re[:, pick], ratio_im[:, pick]
            )
        return total_re[None, :, None], total_im[None, :, None]

    def scale(gain, values):
        moved = complex_multiply(gain[0], gain[1], values[0:1], values[1:2])
        return jnp.concatenate(moved, axis=0)

    first, second = cayley_rows(amplified, diffraction, counter)

    def joined(values, reversed_half):
        if reversed_half is None:
            return values
        return jnp.concatenate([values, jnp.flip(reversed_half, -1)], axis=-1)

    edge_re = jnp.concatenate([green_re[:, 0:1, 1 : block + 1], green_re[:, block + 1 :, 1 : block + 1]], axis=1)
    edge_im = jnp.concatenate([green_im[:, 0:1, 1 : block + 1], green_im[:, block + 1 :, 1 : block + 1]], axis=1)
    edges = joined(
        apply_block(edge_re, edge_im, first),
        None if second is None else apply_block(edge_re, edge_im, second),
    )
    along_y = joined(first, second)
    from_left = shifted(edges[1], "gx", 1)
    from_right = shifted(edges[0], "gx", -1)
    span = 1
    while span < count - 1:
        far_left = shifted(from_left, "gx", span)
        far_right = shifted(from_right, "gx", -span)
        from_left = from_left + scale(span_product(rise_re, rise_im, me - span, span), far_left)
        from_right = from_right + scale(span_product(fall_re, fall_im, me + 1, span), far_right)
        span *= 2

    local = apply_block(
        green_re[:, 1 : block + 1, 1 : block + 1], green_im[:, 1 : block + 1, 1 : block + 1], along_y
    )
    lead_re, lead_im = safe_ratio(
        green_re[:, 1 : block + 1, 0],
        green_im[:, 1 : block + 1, 0],
        green_re[:, 1:2, 0],
        green_im[:, 1:2, 0],
    )
    trail_re, trail_im = safe_ratio(
        green_re[:, 1 : block + 1, block + 1],
        green_im[:, 1 : block + 1, block + 1],
        green_re[:, block : block + 1, block + 1],
        green_im[:, block : block + 1, block + 1],
    )
    lead = complex_multiply(
        lead_re.T[:, :, None], lead_im.T[:, :, None], from_left[None, 0], from_left[None, 1]
    )
    trail = complex_multiply(
        trail_re.T[:, :, None], trail_im.T[:, :, None], from_right[None, 0], from_right[None, 1]
    )
    solved = local + jnp.stack([lead[0] + trail[0], lead[1] + trail[1]], axis=1)
    result = jnp.transpose(2.0 * solved - along_y, (0, 2, 1, 3))

    fluence_out, _ = butterfly_sum(power_sum(result), "wl", ())
    gain_out = base_gain / (1.0 + fluence_out / spectra)
    return (result * jnp.exp(0.5 * gain_out)[:, None, None, :], gain_out)


def solution(mesh):
    placed = (P("gx", "wl", None, None), P("gx", None), P(), P("wl"), P("wl"))
    return jax.shard_map(
        shards,
        mesh=mesh,
        in_specs=placed,
        out_specs=(P("gx", "wl", None, None), P("gx", None)),
        check_vma=False,
    )
```

```python
import math

import jax
import jax.numpy as jnp
from jax import lax
from jax.experimental.layout import Layout, with_layout_constraint
from jax.sharding import PartitionSpec as P

HIGHEST = lax.Precision.HIGHEST
HIGH = lax.Precision.HIGH


def complex_multiply(left_re, left_im, right_re, right_im):
    return (left_re * right_re - left_im * right_im, left_re * right_im + left_im * right_re)


def complex_div(top_re, top_im, bottom_re, bottom_im):
    magnitude = bottom_re * bottom_re + bottom_im * bottom_im
    return (
        (top_re * bottom_re + top_im * bottom_im) / magnitude,
        (top_im * bottom_re - top_re * bottom_im) / magnitude,
    )


def sine_rows(index, length):
    mode = jnp.arange(1, length + 1, dtype=jnp.int32)
    product = ((index + 1)[:, None] * mode[None, :]) % (2 * (length + 1))
    value = jnp.sin(product.astype(jnp.float32) * (math.pi / (length + 1))) * math.sqrt(
        2.0 / (length + 1)
    )
    inside = ((index >= 0) & (index < length))[:, None]
    return jnp.where(inside, value, 0.0)


def eigen_scaled(length, diffraction):
    counter = jnp.arange(1, length + 1, dtype=jnp.float32)
    eigenvalue = 4.0 * jnp.sin(counter * (math.pi / (2 * (length + 1)))) ** 2
    return diffraction[:, None] * eigenvalue[None, :]


def inverse_factor(length, diffraction):
    scaled = eigen_scaled(length, diffraction)
    magnitude = 1.0 + scaled * scaled
    return 1.0 / magnitude, -scaled / magnitude


def butterfly_sum(value, axis, rider):
    count = lax.axis_size(axis)
    if count & (count - 1):
        return lax.optimization_barrier((lax.psum(value, axis), rider))
    step = count // 2
    while step >= 1:
        pairs = [(i, i ^ step) for i in range(count)]
        value = value + lax.ppermute(value, axis, pairs)
        if step == count // 2:
            value, rider = lax.optimization_barrier((value, rider))
        step //= 2
    return value, rider


def shifted(value, axis, offset):
    count = lax.axis_size(axis)
    pairs = [(i, i + offset) for i in range(count) if 0 <= i + offset < count]
    return jax.tree.map(lambda part: lax.ppermute(part, axis, pairs), value)


def green_entries(rows, cols, factor_re, factor_im, length):
    row_table = sine_rows(rows, length)
    col_table = sine_rows(cols, length)
    both = row_table * col_table
    return (
        jnp.einsum("mn,wn->wm", both, factor_re, precision=HIGHEST),
        jnp.einsum("mn,wn->wm", both, factor_im, precision=HIGHEST),
    )


def safe_ratio(top_re, top_im, bottom_re, bottom_im):
    empty = (bottom_re == 0.0) & (bottom_im == 0.0)
    ratio_re, ratio_im = complex_div(
        top_re, top_im, jnp.where(empty, 1.0, bottom_re), bottom_im
    )
    return jnp.where(empty, 0.0, ratio_re), jnp.where(empty, 0.0, ratio_im)


def mode_sines(rows, modes, length):
    product = ((rows + 1)[:, None] * modes[None, :]) % (2 * (length + 1))
    return jnp.sin(product.astype(jnp.float32) * (math.pi / (length + 1))) * math.sqrt(
        2.0 / (length + 1)
    )


def cayley_spectrum(modes, length, diffraction):
    eigenvalue = 4.0 * jnp.sin(modes.astype(jnp.float32) * (math.pi / (2 * (length + 1)))) ** 2
    scaled = diffraction[:, None] * eigenvalue[None, :]
    magnitude = 1.0 + scaled * scaled
    return (1.0 - scaled * scaled) / magnitude, -2.0 * scaled / magnitude


def phased(spectrum, phase_re, phase_im):
    mixed_re, mixed_im = complex_multiply(
        spectrum[..., 0, :, :], spectrum[..., 1, :, :], phase_re, phase_im
    )
    return jnp.stack([mixed_re, mixed_im], axis=-3)


def cayley_rows(values, diffraction, counter):
    length = values.shape[-1]
    if length % 2:
        table = mode_sines(counter, counter + 1, length)
        phase = cayley_spectrum(counter + 1, length, diffraction)
        spectrum = jnp.dot(values, table, precision=HIGH)
        return jnp.dot(phased(spectrum, *phase), table, precision=HIGH), None
    half = length // 2
    rows = counter[:half]
    odd_table = mode_sines(rows, 2 * rows + 1, length)
    even_table = mode_sines(rows, 2 * rows + 2, length)
    low = values[..., :half]
    high = jnp.flip(values[..., half:], -1)
    odd = jnp.dot(low + high, odd_table, precision=HIGH)
    even = jnp.dot(low - high, even_table, precision=HIGH)
    odd = phased(odd, *cayley_spectrum(2 * rows + 1, length, diffraction))
    even = phased(even, *cayley_spectrum(2 * rows + 2, length, diffraction))
    back_odd = jnp.einsum("...q,jq->...j", odd, odd_table, precision=HIGH)
    back_even = jnp.einsum("...q,jq->...j", even, even_table, precision=HIGH)
    return back_odd + back_even, back_odd - back_even


def shards(beam_field, region_labels, gain_table, diffraction, spectral_weight):
    block, spectra_dev, _, columns = beam_field.shape
    spectra = spectra_dev * lax.axis_size("wl")
    count = lax.axis_size("gx")
    me = lax.axis_index("gx")
    cells = block * count
    regions = gain_table.shape[0]
    region_index = jnp.arange(regions, dtype=jnp.int32)
    base_gain = jnp.sum(
        jnp.where(
            region_labels[None] == region_index[:, None, None], gain_table[:, None, None], 0.0
        ),
        axis=0,
    )

    def power_sum(values):
        return jnp.sum(spectral_weight[None, :, None, None] * (values * values), axis=(1, 2))

    fluence_in, counter = butterfly_sum(
        power_sum(beam_field), "wl", jnp.arange(columns, dtype=jnp.int32)
    )
    gain_in = base_gain / (1.0 + fluence_in / spectra)
    amplified = with_layout_constraint(
        jnp.transpose(beam_field, (0, 2, 1, 3)) * jnp.exp(0.5 * gain_in)[:, None, None, :],
        Layout(major_to_minor=(0, 1, 2, 3)),
    )

    factor_re, factor_im = inverse_factor(cells, diffraction)
    start = me * block
    around = start - 1 + jnp.arange(block + 2, dtype=jnp.int32)
    around_table = sine_rows(around, cells)
    green_re = jnp.einsum(
        "an,wn,bn->wab", around_table, factor_re, around_table, precision=HIGHEST
    )
    green_im = jnp.einsum(
        "an,wn,bn->wab", around_table, factor_im, around_table, precision=HIGHEST
    )

    def apply_block(rows_re, rows_im, values):
        kernel = jnp.stack(
            [
                jnp.stack([rows_re, -rows_im], axis=2),
                jnp.stack([rows_im, rows_re], axis=2),
            ],
            axis=1,
        )
        return jnp.einsum("wdack,kcwy->adwy", kernel, values, precision=HIGH)

    block_index = jnp.arange(count, dtype=jnp.int32)
    starts = block_index * block
    ends = starts + block - 1
    rise_re, rise_im = safe_ratio(
        *green_entries(starts + block, starts - 1, factor_re, factor_im, cells),
        *green_entries(starts, starts - 1, factor_re, factor_im, cells),
    )
    fall_re, fall_im = safe_ratio(
        *green_entries(ends - block, ends + 1, factor_re, factor_im, cells),
        *green_entries(ends, ends + 1, factor_re, factor_im, cells),
    )

    def span_product(ratio_re, ratio_im, first, length):
        total_re = jnp.ones_like(ratio_re[:, 0])
        total_im = jnp.zeros_like(ratio_im[:, 0])
        for offset in range(length):
            pick = jnp.clip(first + offset, 0, count - 1)
            total_re, total_im = complex_multiply(
                total_re, total_im, ratio_re[:, pick], ratio_im[:, pick]
            )
        return total_re[None, :, None], total_im[None, :, None]

    def scale(gain, values):
        moved = complex_multiply(gain[0], gain[1], values[0:1], values[1:2])
        return jnp.concatenate(moved, axis=0)

    first, second = cayley_rows(amplified, diffraction, counter)

    def joined(values, reversed_half):
        if reversed_half is None:
            return values
        return jnp.concatenate([values, jnp.flip(reversed_half, -1)], axis=-1)

    edge_re = jnp.concatenate([green_re[:, 0:1, 1 : block + 1], green_re[:, block + 1 :, 1 : block + 1]], axis=1)
    edge_im = jnp.concatenate([green_im[:, 0:1, 1 : block + 1], green_im[:, block + 1 :, 1 : block + 1]], axis=1)
    edges = joined(
        apply_block(edge_re, edge_im, first),
        None if second is None else apply_block(edge_re, edge_im, second),
    )
    along_y = joined(first, second)
    from_left = shifted(edges[1], "gx", 1)
    from_right = shifted(edges[0], "gx", -1)
    span = 1
    while span < count - 1:
        far_left = shifted(from_left, "gx", span)
        far_right = shifted(from_right, "gx", -span)
        from_left = from_left + scale(span_product(rise_re, rise_im, me - span, span), far_left)
        from_right = from_right + scale(span_product(fall_re, fall_im, me + 1, span), far_right)
        span *= 2

    local = apply_block(
        green_re[:, 1 : block + 1, 1 : block + 1], green_im[:, 1 : block + 1, 1 : block + 1], along_y
    )
    lead_re, lead_im = safe_ratio(
        green_re[:, 1 : block + 1, 0],
        green_im[:, 1 : block + 1, 0],
        green_re[:, 1:2, 0],
        green_im[:, 1:2, 0],
    )
    trail_re, trail_im = safe_ratio(
        green_re[:, 1 : block + 1, block + 1],
        green_im[:, 1 : block + 1, block + 1],
        green_re[:, block : block + 1, block + 1],
        green_im[:, block : block + 1, block + 1],
    )
    lead = complex_multiply(
        lead_re.T[:, :, None], lead_im.T[:, :, None], from_left[None, 0], from_left[None, 1]
    )
    trail = complex_multiply(
        trail_re.T[:, :, None], trail_im.T[:, :, None], from_right[None, 0], from_right[None, 1]
    )
    solved = local + jnp.stack([lead[0] + trail[0], lead[1] + trail[1]], axis=1)
    result = jnp.transpose(2.0 * solved - along_y, (0, 2, 1, 3))

    fluence_out, _ = butterfly_sum(power_sum(result), "wl", ())
    gain_out = base_gain / (1.0 + fluence_out / spectra)
    return (result * jnp.exp(0.5 * gain_out)[:, None, None, :], gain_out)


def solution(mesh):
    placed = (P("gx", "wl", None, None), P("gx", None), P(), P("wl"), P("wl"))
    return jax.shard_map(
        shards,
        mesh=mesh,
        in_specs=placed,
        out_specs=(P("gx", "wl", None, None), P("gx", None)),
        check_vma=False,
    )
```
